512 devices in a mesh: cfg: 2 (over core), grp: 4 (over y), seq: 64 (over x, z).
Axes of the slice: x: 4, y: 4, z: 16, core: 2. Of those that a mesh axis runs over, the one named last changes fastest.
Arguments:
- query: bfloat16 [2, 4, 2, 128, 2432], P('cfg', 'grp', None, 'seq'), may hold values from -150 to 150
- keys: bfloat16 [2, 4, 2, 128, 2432], P('cfg', 'grp', None, 'seq'), may hold values from -5.5 to 5.5
- values: bfloat16 [2, 4, 2, 128, 2432], P('cfg', 'grp', None, 'seq'), may hold values from -5 to 5
- hidden: bfloat16 [2, 4, 2, 128, 2432], P('cfg', 'grp', None, 'seq'), may hold values from -23 to 23
- latent: float32 [4, 2, 128, 64], P('grp', None, 'seq', 'cfg'), may hold values from -6 to 6
- deal: int32 [4, 2], replicated, may hold values from 0 to 5, as said below
- lengths: int32 [4, 2], replicated, may hold values from 64 to 128, as said below
- w_out: bfloat16 [2432, 2432], P(('cfg', 'seq')), may hold values from -0.125 to 0.125
- attn_gate: float32 [2, 6, 2432], P('cfg'), may hold values from 0.25 to 1.75
- modulation: float32 [2, 6, 2, 2432], P('cfg'), may hold values from -3 to 3
- w_final: bfloat16 [2432, 64], replicated, may hold values from -0.125 to 0.125
- guide: float32 [6], replicated, may hold values from 2 to 7
- step_size: float32 [6], replicated, may hold values from 0.15 to 0.5
Outputs:
- latent_next: float32 [4, 2, 128, 64], P('grp', None, 'seq', 'cfg')
The draws below stay inside these ranges and needn't reach their ends.
Inputs may be any that keep to these rules, and one draw needn't show every extreme that they name: `deal`: column 0 of row g names the whole item of group g, column 1 the item split between groups g and g xor 1 (equal in both rows); every one of the 6 items is named by exactly one column-0 entry or one pair of column-1 entries. `lengths`: in each column some group has all 128 slots live.
All inputs are finite; a program needn't handle non-finite values.
Results may differ from the reference program's by a relative error of at most 0.0049.
Values may be sent and summed in bfloat16 or wider, within the bound.
No kernel may reach another device: no remote copies, remote signals or barrier semaphores. Data moves between devices by JAX's collectives and lax.ppermute only.
A program may use at most 128 MiB of HBM per device.

```python
import jax
import jax.numpy as jnp
from jax import lax

D = 2432
HEADS = 38
HD = 64
CH = 64
SLOTS = 128
GROUPS = 4
BRANCHES = 2
ITEMS = 6


def key_tensor_field(key):
    field_shape = (BRANCHES, GROUPS, 2, SLOTS, D)
    field = jnp.clip(jax.random.normal(jax.random.fold_in(key, 11), field_shape, jnp.float32), -5.0, 5.0)
    return field


def draw_keys(key, part):
    return key_tensor_field(key).astype(jnp.bfloat16)


def draw_query(key, part):
    field_shape = (BRANCHES, GROUPS, 2, SLOTS, D)
    result = jnp.clip(jax.random.normal(jax.random.fold_in(key, 21), field_shape, jnp.float32), -5.0, 5.0) * 3.0
    return result.astype(jnp.bfloat16)


def draw_hidden(key, part):
    field_shape = (BRANCHES, GROUPS, 2, SLOTS, D)
    field = jnp.clip(jax.random.normal(jax.random.fold_in(key, 31), field_shape, jnp.float32), -5.0, 5.0)
    row_scale = jnp.exp(jax.random.uniform(jax.random.fold_in(key, 32), (BRANCHES, GROUPS, 2, SLOTS, 1), jnp.float32, -1.9, 0.4))
    col_scale = jnp.exp(jax.random.uniform(jax.random.fold_in(key, 33), (D,), jnp.float32, -1.2, 1.09))
    return (field * row_scale * col_scale).astype(jnp.bfloat16)


def draw_deal(key, part):
    shuffled = jax.random.permutation(jax.random.fold_in(key, 51), ITEMS).astype(jnp.int32)
    group_ids = jnp.arange(GROUPS)
    home_items = shuffled[group_ids]
    split_items = shuffled[GROUPS + group_ids // 2]
    return jnp.stack([home_items, split_items], axis=1).astype(jnp.int32)


def draw_lengths(key, part):
    live_counts = jax.random.randint(jax.random.fold_in(key, 41), (GROUPS, 2), SLOTS // 2, SLOTS + 1)
    full_group = jax.random.randint(jax.random.fold_in(key, 42), (2,), 0, GROUPS)
    group_ids = jnp.arange(GROUPS)
    live_counts = jnp.where(group_ids[:, None] == full_group[None, :], SLOTS, live_counts)
    return live_counts.astype(jnp.int32)


def shard_levels(key, dims, cuts, low, high):
    factor_of = 1.0
    for position, shards_of in cuts:
        draws = jax.random.uniform(jax.random.fold_in(jax.random.fold_in(key, 6), position), (shards_of,), jnp.float32, low / len(cuts), high / len(cuts))
        factor_of = factor_of * jnp.repeat(jnp.exp(draws), dims[position] // shards_of).reshape((-1,) + (1,) * (len(dims) - 1 - position))
    return factor_of


def noise(key, shape, width, limit, cuts=(), dtype=jnp.bfloat16):
    entries = jax.random.normal(key, shape, jnp.float32) * width
    if len(cuts) > 0:
        entries = shard_levels(key, shape, cuts, -0.22, 0.18) * entries
    return jnp.clip(entries, min=-limit, max=limit).astype(dtype)


def setup_inputs(seed: int = 0) -> dict:
    key_of = jax.random.split(jax.random.key(seed), 14)
    query = draw_query(jax.random.fold_in(key_of[13], 71), 0)
    keys = draw_keys(jax.random.fold_in(key_of[13], 71), 0)
    values = noise(key_of[2], (BRANCHES, GROUPS, 2, SLOTS, D), 1.0, 5.0, ((0, 2), (1, 4), (3, 64)))
    hidden = draw_hidden(jax.random.fold_in(key_of[13], 71), 0)
    latent = noise(key_of[4], (GROUPS, 2, SLOTS, CH), 1.0, 6.0, ((0, 4), (2, 64), (3, 2)), jnp.float32)
    deal = draw_deal(jax.random.fold_in(key_of[13], 71), 0)
    lengths = draw_lengths(jax.random.fold_in(key_of[13], 71), 0)
    w_out = noise(key_of[7], (D, D), D ** -0.5, 0.125, ((0, 128),))
    attn_gate = jnp.clip(1.0 + 0.15 * jax.random.normal(key_of[8], (BRANCHES, ITEMS, D), jnp.float32), 0.25, 1.75)
    modulation = noise(key_of[9], (BRANCHES, ITEMS, 2, D), 0.5, 3.0, ((0, 2),), jnp.float32)
    w_final = noise(key_of[10], (D, CH), D ** -0.5, 0.125)
    guide = jnp.clip(jax.random.uniform(key_of[11], (ITEMS,), jnp.float32, 2.0, 7.0), 2.0, 7.0)
    step_size = jnp.clip(jax.random.uniform(key_of[12], (ITEMS,), jnp.float32, 0.15, 0.5), 0.15, 0.5)
    return dict(query=query, keys=keys, values=values, hidden=hidden, latent=latent, deal=deal, lengths=lengths, w_out=w_out, attn_gate=attn_gate, modulation=modulation, w_final=w_final, guide=guide, step_size=step_size)


NORM_EPS = 1e-06

def attend(queries, keys_all, values_all, live_keys):
    row_count = queries.shape[0]
    query_heads = queries.astype(jnp.float32).reshape(row_count, HEADS, HD)
    key_heads = keys_all.astype(jnp.float32).reshape(-1, HEADS, HD)
    value_heads = values_all.astype(jnp.float32).reshape(-1, HEADS, HD)
    scores = jnp.einsum('shd,khd->hsk', query_heads, key_heads) * HD ** (-0.5)
    scores = jnp.where(live_keys[None, None, :], scores, -jnp.inf)
    peak_score = lax.optimization_barrier(jnp.max(scores, axis=2, keepdims=True))
    raw_weights = jnp.exp(scores - peak_score)
    row_total = lax.optimization_barrier(jnp.sum(raw_weights, axis=2, keepdims=True))
    weights = raw_weights.astype(jnp.bfloat16).astype(jnp.float32)
    mixed_out = jnp.einsum('hsk,khd->hsd', weights, value_heads) / row_total
    return jnp.transpose(mixed_out, (1, 0, 2)).reshape(row_count, HEADS * HD)

def reference(query, keys, values, hidden, latent, deal, lengths, w_out, attn_gate, modulation, w_final, guide, step_size):
    slot_ids = jnp.arange(SLOTS)
    results = []
    for group_id in range(GROUPS):
        partner = group_id ^ 1
        live_home = slot_ids < lengths[group_id, 0]
        live_own = slot_ids < lengths[group_id, 1]
        live_pair = slot_ids < lengths[partner, 1]
        item_ids = deal[group_id]
        branch_velocity = []
        for branch in range(BRANCHES):
            local_output_rows = attend(query[branch, group_id, 0], keys[branch, group_id, 0], values[branch, group_id, 0], live_home)
            shared = attend(query[branch, group_id, 1], jnp.concatenate([keys[branch, group_id, 1], keys[branch, partner, 1]], 0), jnp.concatenate([values[branch, group_id, 1], values[branch, partner, 1]], 0), jnp.concatenate([live_own, live_pair], 0))
            attn = jnp.stack([local_output_rows, shared]).astype(jnp.bfloat16)
            projected = jnp.dot(attn.reshape(-1, D), w_out, preferred_element_type=jnp.float32).reshape(2, SLOTS, D)
            gate_now = attn_gate[branch][item_ids]
            stream = hidden[branch, group_id].astype(jnp.float32) + gate_now[:, None, :] * projected
            row_mean = lax.optimization_barrier(jnp.mean(stream, axis=2, keepdims=True))
            centred = stream - row_mean
            row_var = lax.optimization_barrier(jnp.mean(centred * centred, axis=2, keepdims=True))
            normed = centred * lax.rsqrt(row_var + NORM_EPS)
            selected_entries = modulation[branch][item_ids]
            shaped = (normed * (1.0 + selected_entries[:, 1][:, None, :]) + selected_entries[:, 0][:, None, :]).astype(jnp.bfloat16)
            velocity = jnp.dot(shaped.reshape(-1, D), w_final, preferred_element_type=jnp.float32).reshape(2, SLOTS, CH)
            live_rows = jnp.stack([live_home, live_own])
            velocity = jnp.where(live_rows[:, :, None], velocity, jnp.float32(0.0))
            branch_velocity.append(velocity)
        weight_now = guide[item_ids][:, None, None]
        guided = branch_velocity[1] + weight_now * (branch_velocity[0] - branch_velocity[1])
        results.append(latent[group_id] - step_size[item_ids][:, None, None] * guided)
    return jnp.stack(results)
```

```python
import jax
import jax.numpy as jnp
from jax import lax
from jax.sharding import PartitionSpec as P

D = 2432
HEADS = 38
HD = 64


NORM_EPS = 1e-06


def from_partner(x, axis, apart):
    return lax.ppermute(x, axis, [(i, i ^ 1 << apart) for i in range(lax.axis_size(axis))])


def head_attend(queries, keys_all, values_all, live_keys):
    scores = jnp.einsum(
        "sd,kd->sk", queries, keys_all, preferred_element_type=jnp.float32
    ) * HD ** (-0.5)
    scores = jnp.where(live_keys[None, :], scores, -jnp.inf)
    peak_score = jnp.max(scores, axis=1, keepdims=True)
    raw_weights = jnp.exp(scores - peak_score)
    row_total = jnp.sum(raw_weights, axis=1, keepdims=True)
    weights = raw_weights.astype(jnp.bfloat16)
    return (
        jnp.einsum("sk,kd->sd", weights, values_all, preferred_element_type=jnp.float32)
        / row_total
    )


def shards(
    query,
    keys,
    values,
    hidden,
    latent,
    deal,
    lengths,
    w_out,
    attn_gate,
    modulation,
    w_final,
    guide,
    step_size,
):
    nseq = lax.axis_size("seq")
    group_id = lax.axis_index("grp")
    branch = lax.axis_index("cfg")
    partner = jnp.bitwise_xor(group_id, 1)
    own_lengths = lax.dynamic_index_in_dim(lengths, group_id, 0, keepdims=False)
    pair_lengths = lax.dynamic_index_in_dim(lengths, partner, 0, keepdims=False)
    item_ids = lax.dynamic_index_in_dim(deal, group_id, 0, keepdims=False)
    local_query = query[0, 0]
    resident_key_rows = keys[0, 0]
    local_values = values[0, 0]
    shard_rows = resident_key_rows.shape[1]
    slot_total = nseq * shard_rows
    far_keys, far_values = from_partner((resident_key_rows[1], local_values[1]), "grp", 0)

    def to_heads(x):
        n = x.shape[0]
        x = x.reshape(n, shard_rows, HEADS, HD).transpose(2, 0, 1, 3)
        return jnp.pad(x, ((0, nseq - HEADS), (0, 0), (0, 0), (0, 0)))

    packed = jnp.concatenate(
        [
            to_heads(local_query),
            to_heads(jnp.concatenate([resident_key_rows, far_keys[None]], 0)),
            to_heads(jnp.concatenate([local_values, far_values[None]], 0)),
        ],
        axis=1,
    )
    head_rows = lax.all_to_all(packed, "seq", 0, 0, tiled=True)
    head_rows = head_rows.transpose(1, 0, 2, 3).reshape(8, slot_total, HD)
    head_q, head_k, head_v = head_rows[0:2], head_rows[2:5], head_rows[5:8]
    slot_ids = jnp.arange(slot_total)
    live_home = slot_ids < own_lengths[0]
    live_own = slot_ids < own_lengths[1]
    live_pair = slot_ids < pair_lengths[1]
    home_out = head_attend(head_q[0], head_k[0], head_v[0], live_home)
    shared_out = head_attend(
        head_q[1],
        jnp.concatenate([head_k[1], head_k[2]], 0),
        jnp.concatenate([head_v[1], head_v[2]], 0),
        jnp.concatenate([live_own, live_pair], 0),
    )
    head_attn = jnp.stack([home_out, shared_out]).astype(jnp.bfloat16)

    every_head = lax.all_to_all(
        jnp.broadcast_to(head_attn[None], (nseq,) + head_attn.shape), "seq", 0, 0, tiled=True
    )
    attn_rows = every_head[:HEADS].transpose(1, 2, 0, 3).reshape(2 * slot_total, D)

    block_rows = w_out.shape[0]
    col_width = D // nseq
    w_parts = w_out.reshape(block_rows, nseq, col_width).transpose(1, 0, 2)
    w_half = lax.all_to_all(w_parts, "seq", 0, 0, tiled=True).reshape(nseq * block_rows, col_width)
    w_other = from_partner(w_half, "cfg", 0)
    w_cols = jnp.where(
        branch == 0,
        jnp.concatenate([w_half, w_other], 0),
        jnp.concatenate([w_other, w_half], 0),
    )
    projected_cols = jnp.dot(attn_rows, w_cols, preferred_element_type=jnp.float32)
    projected_parts = projected_cols.reshape(2, nseq, shard_rows, col_width).transpose(1, 0, 2, 3)
    projected = lax.all_to_all(projected_parts, "seq", 0, 0, tiled=True)
    projected = projected.transpose(1, 2, 0, 3).reshape(2, shard_rows, D)

    item_count = guide.shape[0]
    indicator_mask = (jnp.arange(item_count)[None, :] == item_ids[:, None]).astype(jnp.float32)
    gate_now = jnp.einsum(
        "ri,id->rd", indicator_mask, attn_gate[0], precision=lax.Precision.HIGHEST
    )
    stream = hidden[0, 0].astype(jnp.float32) + gate_now[:, None, :] * projected
    row_mean = jnp.mean(stream, axis=2, keepdims=True)
    centred = stream - row_mean
    row_var = jnp.mean(centred * centred, axis=2, keepdims=True)
    normed = centred * lax.rsqrt(row_var + NORM_EPS)
    selected_entries = jnp.einsum(
        "ub,bkg->ukg", indicator_mask, modulation[0], precision=lax.Precision.HIGHEST
    )
    shaped = (
        normed * (1.0 + selected_entries[:, 1][:, None, :]) + selected_entries[:, 0][:, None, :]
    ).astype(jnp.bfloat16)
    velocity = jnp.einsum("rsd,dc->rsc", shaped, w_final, preferred_element_type=jnp.float32)
    row_slots = lax.axis_index("seq") * shard_rows + jnp.arange(shard_rows)
    live_rows = jnp.stack([row_slots < own_lengths[0], row_slots < own_lengths[1]])
    velocity = jnp.where(live_rows[:, :, None], velocity, jnp.float32(0.0))
    weight_now = jnp.sum(indicator_mask * guide[None, :], axis=1)[:, None, None]
    step_now = jnp.sum(indicator_mask * step_size[None, :], axis=1)[:, None, None]
    latent_part = latent[0]
    part_width = latent_part.shape[2]
    outgoing_velocity = lax.dynamic_slice_in_dim(velocity, (1 - branch) * part_width, part_width, 2)
    own_velocity = lax.dynamic_slice_in_dim(velocity, branch * part_width, part_width, 2)
    other_velocity = from_partner(outgoing_velocity, "cfg", 0)
    is_conditional = branch == 0
    cond_velocity = jnp.where(is_conditional, own_velocity, other_velocity)
    uncond_velocity = jnp.where(is_conditional, other_velocity, own_velocity)
    guided = uncond_velocity + weight_now * (cond_velocity - uncond_velocity)
    updated = latent_part - step_now * guided
    return updated[None]


def solution(mesh):
    placed = (
        P("cfg", "grp", None, "seq", None),
        P("cfg", "grp", None, "seq", None),
        P("cfg", "grp", None, "seq", None),
        P("cfg", "grp", None, "seq", None),
        P("grp", None, "seq", "cfg"),
        P(),
        P(),
        P(("cfg", "seq"), None),
        P("cfg", None, None),
        P("cfg", None, None, None),
        P(),
        P(),
        P(),
    )
    return jax.shard_map(
        shards, mesh=mesh, in_specs=placed, out_specs=P("grp", None, "seq", "cfg"), check_vma=False
    )
```

```python
import jax
import jax.numpy as jnp
from jax import lax
from jax.sharding import PartitionSpec as P

D = 2432
HEADS = 38
HD = 64


NORM_EPS = 1e-06


def from_partner(x, axis, apart):
    return lax.ppermute(x, axis, [(i, i ^ 1 << apart) for i in range(lax.axis_size(axis))])


def head_attend(queries, keys_all, values_all, live_keys):
    scores = jnp.einsum(
        "sd,kd->sk", queries, keys_all, preferred_element_type=jnp.float32
    ) * HD ** (-0.5)
    scores = jnp.where(live_keys[None, :], scores, -jnp.inf)
    peak_score = jnp.max(scores, axis=1, keepdims=True)
    raw_weights = jnp.exp(scores - peak_score)
    row_total = jnp.sum(raw_weights, axis=1, keepdims=True)
    weights = raw_weights.astype(jnp.bfloat16)
    return (
        jnp.einsum("sk,kd->sd", weights, values_all, preferred_element_type=jnp.float32)
        / row_total
    )


def butterfly_bits(n):
    bits = [b for b in range(n.bit_length() - 1)]
    return sorted(bits, key=lambda b: -hop_distance(b))


def hop_distance(bit):
    z_bits = 4
    span = 16 if bit < z_bits else 4
    step = 1 << (bit if bit < z_bits else bit - z_bits)
    return min(step, span - step)


def shards(
    query,
    keys,
    values,
    hidden,
    latent,
    deal,
    lengths,
    w_out,
    attn_gate,
    modulation,
    w_final,
    guide,
    step_size,
):
    nseq = lax.axis_size("seq")
    group_id = lax.axis_index("grp")
    branch = lax.axis_index("cfg")
    partner = jnp.bitwise_xor(group_id, 1)
    own_lengths = lax.dynamic_index_in_dim(lengths, group_id, 0, keepdims=False)
    pair_lengths = lax.dynamic_index_in_dim(lengths, partner, 0, keepdims=False)
    item_ids = lax.dynamic_index_in_dim(deal, group_id, 0, keepdims=False)
    local_query = query[0, 0]
    resident_key_rows = keys[0, 0]
    local_values = values[0, 0]
    shard_rows = resident_key_rows.shape[1]
    slot_total = nseq * shard_rows
    far_keys, far_values = from_partner((resident_key_rows[1], local_values[1]), "grp", 0)

    def to_heads(x):
        n = x.shape[0]
        x = x.reshape(n, shard_rows, HEADS, HD).transpose(2, 0, 1, 3)
        return jnp.pad(x, ((0, nseq - HEADS), (0, 0), (0, 0), (0, 0)))

    block_rows = w_out.shape[0]
    col_width = D // nseq
    w_parts = w_out.reshape(block_rows, nseq, col_width).transpose(1, 0, 2)
    packed = jnp.concatenate(
        [
            to_heads(local_query),
            to_heads(jnp.concatenate([resident_key_rows, far_keys[None]], 0)),
            to_heads(jnp.concatenate([local_values, far_values[None]], 0)),
        ],
        axis=1,
    )
    head_width = packed.shape[1] * shard_rows * HD
    joint = jnp.concatenate(
        [packed.reshape(nseq, head_width), w_parts.reshape(nseq, block_rows * col_width)], 1
    )
    joint = lax.all_to_all(joint, "seq", 0, 0, tiled=True)
    head_rows = joint[:, :head_width].reshape(nseq, 8, shard_rows, HD)
    head_rows = head_rows.transpose(1, 0, 2, 3).reshape(8, slot_total, HD)
    head_q, head_k, head_v = head_rows[0:2], head_rows[2:5], head_rows[5:8]
    slot_ids = jnp.arange(slot_total)
    live_home = slot_ids < own_lengths[0]
    live_own = slot_ids < own_lengths[1]
    live_pair = slot_ids < pair_lengths[1]
    home_out = head_attend(head_q[0], head_k[0], head_v[0], live_home)
    shared_out = head_attend(
        head_q[1],
        jnp.concatenate([head_k[1], head_k[2]], 0),
        jnp.concatenate([head_v[1], head_v[2]], 0),
        jnp.concatenate([live_own, live_pair], 0),
    )
    head_attn = jnp.stack([home_out, shared_out]).astype(jnp.bfloat16)

    w_half = joint[:, head_width:].reshape(nseq * block_rows, col_width)
    w_other = from_partner(w_half, "cfg", 0)
    w_cols = jnp.where(
        branch == 0,
        jnp.concatenate([w_half, w_other], 0),
        jnp.concatenate([w_other, w_half], 0),
    )

    me = lax.axis_index("seq")
    gathered = head_attn[None]
    masks = [0]
    for bit in butterfly_bits(nseq):
        gathered = jnp.concatenate([gathered, from_partner(gathered, "seq", bit)], 0)
        masks = masks + [m ^ (1 << bit) for m in masks]
    source_head = jnp.bitwise_xor(me, jnp.array(masks, jnp.int32))
    w_heads = jnp.pad(
        w_cols.reshape(HEADS, HD, col_width), ((0, nseq - HEADS), (0, 0), (0, 0))
    )
    w_ordered = jnp.take(w_heads, source_head, axis=0)
    projected_cols = jnp.einsum(
        "irsd,idc->rsc", gathered, w_ordered, preferred_element_type=jnp.float32
    ).reshape(2 * slot_total, col_width)
    projected_parts = projected_cols.reshape(2, nseq, shard_rows, col_width).transpose(1, 0, 2, 3)
    projected = lax.all_to_all(projected_parts, "seq", 0, 0, tiled=True)
    projected = projected.transpose(1, 2, 0, 3).reshape(2, shard_rows, D)

    item_count = guide.shape[0]
    indicator_mask = (jnp.arange(item_count)[None, :] == item_ids[:, None]).astype(jnp.float32)
    gate_now = jnp.einsum(
        "ri,id->rd", indicator_mask, attn_gate[0], precision=lax.Precision.HIGHEST
    )
    stream = hidden[0, 0].astype(jnp.float32) + gate_now[:, None, :] * projected
    row_mean = jnp.mean(stream, axis=2, keepdims=True)
    centred = stream - row_mean
    row_var = jnp.mean(centred * centred, axis=2, keepdims=True)
    normed = centred * lax.rsqrt(row_var + NORM_EPS)
    selected_entries = jnp.einsum(
        "ub,bkg->ukg", indicator_mask, modulation[0], precision=lax.Precision.HIGHEST
    )
    shaped = (
        normed * (1.0 + selected_entries[:, 1][:, None, :]) + selected_entries[:, 0][:, None, :]
    ).astype(jnp.bfloat16)
    velocity = jnp.einsum("rsd,dc->rsc", shaped, w_final, preferred_element_type=jnp.float32)
    row_slots = lax.axis_index("seq") * shard_rows + jnp.arange(shard_rows)
    live_rows = jnp.stack([row_slots < own_lengths[0], row_slots < own_lengths[1]])
    velocity = jnp.where(live_rows[:, :, None], velocity, jnp.float32(0.0))
    weight_now = jnp.sum(indicator_mask * guide[None, :], axis=1)[:, None, None]
    step_now = jnp.sum(indicator_mask * step_size[None, :], axis=1)[:, None, None]
    latent_part = latent[0]
    part_width = latent_part.shape[2]
    outgoing_velocity = lax.dynamic_slice_in_dim(velocity, (1 - branch) * part_width, part_width, 2)
    own_velocity = lax.dynamic_slice_in_dim(velocity, branch * part_width, part_width, 2)
    other_velocity = from_partner(outgoing_velocity, "cfg", 0)
    is_conditional = branch == 0
    cond_velocity = jnp.where(is_conditional, own_velocity, other_velocity)
    uncond_velocity = jnp.where(is_conditional, other_velocity, own_velocity)
    guided = uncond_velocity + weight_now * (cond_velocity - uncond_velocity)
    updated = latent_part - step_now * guided
    return updated[None]


def solution(mesh):
    placed = (
        P("cfg", "grp", None, "seq", None),
        P("cfg", "grp", None, "seq", None),
        P("cfg", "grp", None, "seq", None),
        P("cfg", "grp", None, "seq", None),
        P("grp", None, "seq", "cfg"),
        P(),
        P(),
        P(("cfg", "seq"), None),
        P("cfg", None, None),
        P("cfg", None, None, None),
        P(),
        P(),
        P(),
    )
    return jax.shard_map(
        shards, mesh=mesh, in_specs=placed, out_specs=P("grp", None, "seq", "cfg"), check_vma=False
    )
```

```python
import jax
import jax.numpy as jnp
from jax import lax
from jax.sharding import PartitionSpec as P

D = 2432
HEADS = 38
HD = 64


NORM_EPS = 1e-06


def from_partner(x, axis, apart):
    return lax.ppermute(x, axis, [(i, i ^ 1 << apart) for i in range(lax.axis_size(axis))])


def head_attend(queries, keys_all, values_all, live_keys):
    scores = jnp.einsum(
        "sd,kd->sk", queries, keys_all, preferred_element_type=jnp.float32
    ) * HD ** (-0.5)
    scores = jnp.where(live_keys[None, :], scores, -jnp.inf)
    peak_score = jnp.max(scores, axis=1, keepdims=True)
    raw_weights = jnp.exp(scores - peak_score)
    row_total = jnp.sum(raw_weights, axis=1, keepdims=True)
    weights = raw_weights.astype(jnp.bfloat16)
    return (
        jnp.einsum("sk,kd->sd", weights, values_all, preferred_element_type=jnp.float32)
        / row_total
    )


def butterfly_orders(n):
    assert n == 64
    return [[3, 2, 1, 5, 0, 4], [2, 3, 5, 1, 4, 0]]


def hop_distance(bit):
    z_bits = 4
    span = 16 if bit < z_bits else 4
    step = 1 << (bit if bit < z_bits else bit - z_bits)
    return min(step, span - step)


def shards(
    query,
    keys,
    values,
    hidden,
    latent,
    deal,
    lengths,
    w_out,
    attn_gate,
    modulation,
    w_final,
    guide,
    step_size,
):
    nseq = lax.axis_size("seq")
    group_id = lax.axis_index("grp")
    branch = lax.axis_index("cfg")
    partner = jnp.bitwise_xor(group_id, 1)
    own_lengths = lax.dynamic_index_in_dim(lengths, group_id, 0, keepdims=False)
    pair_lengths = lax.dynamic_index_in_dim(lengths, partner, 0, keepdims=False)
    item_ids = lax.dynamic_index_in_dim(deal, group_id, 0, keepdims=False)
    local_query = query[0, 0]
    resident_key_rows = keys[0, 0]
    local_values = values[0, 0]
    shard_rows = resident_key_rows.shape[1]
    slot_total = nseq * shard_rows
    far_keys, far_values = from_partner((resident_key_rows[1], local_values[1]), "grp", 0)

    def to_heads(x):
        n = x.shape[0]
        x = x.reshape(n, shard_rows, HEADS, HD).transpose(2, 0, 1, 3)
        return jnp.pad(x, ((0, nseq - HEADS), (0, 0), (0, 0), (0, 0)))

    block_rows = w_out.shape[0]
    col_width = D // nseq
    w_parts = w_out.reshape(block_rows, nseq, col_width).transpose(1, 0, 2)
    packed = jnp.concatenate(
        [
            to_heads(local_query),
            to_heads(jnp.concatenate([resident_key_rows, far_keys[None]], 0)),
            to_heads(jnp.concatenate([local_values, far_values[None]], 0)),
        ],
        axis=1,
    )
    head_width = packed.shape[1] * shard_rows * HD
    joint = jnp.concatenate(
        [packed.reshape(nseq, head_width), w_parts.reshape(nseq, block_rows * col_width)], 1
    )
    joint = lax.all_to_all(joint, "seq", 0, 0, tiled=True)
    head_rows = joint[:, :head_width].reshape(nseq, 8, shard_rows, HD)
    head_rows = head_rows.transpose(1, 0, 2, 3).reshape(8, slot_total, HD)
    head_q, head_k, head_v = head_rows[0:2], head_rows[2:5], head_rows[5:8]
    slot_ids = jnp.arange(slot_total)
    live_home = slot_ids < own_lengths[0]
    live_own = slot_ids < own_lengths[1]
    live_pair = slot_ids < pair_lengths[1]
    home_out = head_attend(head_q[0], head_k[0], head_v[0], live_home)
    shared_out = head_attend(
        head_q[1],
        jnp.concatenate([head_k[1], head_k[2]], 0),
        jnp.concatenate([head_v[1], head_v[2]], 0),
        jnp.concatenate([live_own, live_pair], 0),
    )
    head_attn = jnp.stack([home_out, shared_out]).astype(jnp.bfloat16)

    w_half = joint[:, head_width:].reshape(nseq * block_rows, col_width)
    w_other = from_partner(w_half, "cfg", 0)
    w_cols = jnp.where(
        branch == 0,
        jnp.concatenate([w_half, w_other], 0),
        jnp.concatenate([w_other, w_half], 0),
    )

    me = lax.axis_index("seq")
    orders = butterfly_orders(nseq)
    gathered = head_attn[None]
    masks = [[0], [0]]
    for step in range(len(orders[0])):
        pairs = [
            (c * nseq + s, c * nseq + (s ^ (1 << orders[c][step])))
            for c in range(2)
            for s in range(nseq)
        ]
        received = lax.ppermute(gathered, ("cfg", "seq"), pairs)
        gathered = jnp.concatenate([gathered, received], 0)
        masks = [m + [x ^ (1 << orders[c][step]) for x in m] for c, m in enumerate(masks)]
    mask_now = jnp.where(branch == 0, jnp.array(masks[0], jnp.int32), jnp.array(masks[1], jnp.int32))
    source_head = jnp.bitwise_xor(me, mask_now)
    w_heads = jnp.pad(
        w_cols.reshape(HEADS, HD, col_width), ((0, nseq - HEADS), (0, 0), (0, 0))
    )
    w_ordered = jnp.take(w_heads, source_head, axis=0)
    projected_cols = jnp.einsum(
        "irsd,idc->rsc", gathered, w_ordered, preferred_element_type=jnp.float32
    ).reshape(2 * slot_total, col_width)
    projected_parts = projected_cols.reshape(2, nseq, shard_rows, col_width).transpose(1, 0, 2, 3)
    projected = lax.all_to_all(projected_parts, "seq", 0, 0, tiled=True)
    projected = projected.transpose(1, 2, 0, 3).reshape(2, shard_rows, D)

    item_count = guide.shape[0]
    indicator_mask = (jnp.arange(item_count)[None, :] == item_ids[:, None]).astype(jnp.float32)
    gate_now = jnp.einsum(
        "ri,id->rd", indicator_mask, attn_gate[0], precision=lax.Precision.HIGHEST
    )
    stream = hidden[0, 0].astype(jnp.float32) + gate_now[:, None, :] * projected
    row_mean = jnp.mean(stream, axis=2, keepdims=True)
    centred = stream - row_mean
    row_var = jnp.mean(centred * centred, axis=2, keepdims=True)
    normed = centred * lax.rsqrt(row_var + NORM_EPS)
    selected_entries = jnp.einsum(
        "ub,bkg->ukg", indicator_mask, modulation[0], precision=lax.Precision.HIGHEST
    )
    shaped = (
        normed * (1.0 + selected_entries[:, 1][:, None, :]) + selected_entries[:, 0][:, None, :]
    ).astype(jnp.bfloat16)
    velocity = jnp.einsum("rsd,dc->rsc", shaped, w_final, preferred_element_type=jnp.float32)
    row_slots = lax.axis_index("seq") * shard_rows + jnp.arange(shard_rows)
    live_rows = jnp.stack([row_slots < own_lengths[0], row_slots < own_lengths[1]])
    velocity = jnp.where(live_rows[:, :, None], velocity, jnp.float32(0.0))
    weight_now = jnp.sum(indicator_mask * guide[None, :], axis=1)[:, None, None]
    step_now = jnp.sum(indicator_mask * step_size[None, :], axis=1)[:, None, None]
    latent_part = latent[0]
    part_width = latent_part.shape[2]
    outgoing_velocity = lax.dynamic_slice_in_dim(velocity, (1 - branch) * part_width, part_width, 2)
    own_velocity = lax.dynamic_slice_in_dim(velocity, branch * part_width, part_width, 2)
    other_velocity = from_partner(outgoing_velocity, "cfg", 0)
    is_conditional = branch == 0
    cond_velocity = jnp.where(is_conditional, own_velocity, other_velocity)
    uncond_velocity = jnp.where(is_conditional, other_velocity, own_velocity)
    guided = uncond_velocity + weight_now * (cond_velocity - uncond_velocity)
    updated = latent_part - step_now * guided
    return updated[None]


def solution(mesh):
    placed = (
        P("cfg", "grp", None, "seq", None),
        P("cfg", "grp", None, "seq", None),
        P("cfg", "grp", None, "seq", None),
        P("cfg", "grp", None, "seq", None),
        P("grp", None, "seq", "cfg"),
        P(),
        P(),
        P(("cfg", "seq"), None),
        P("cfg", None, None),
        P("cfg", None, None, None),
        P(),
        P(),
        P(),
    )
    return jax.shard_map(
        shards, mesh=mesh, in_specs=placed, out_specs=P("grp", None, "seq", "cfg"), check_vma=False
    )
```

```python
import jax
import jax.numpy as jnp
from jax import lax
from jax.sharding import PartitionSpec as P

D = 2432
HEADS = 38
HD = 64


NORM_EPS = 1e-06


def from_partner(x, axis, apart):
    return lax.ppermute(x, axis, [(i, i ^ 1 << apart) for i in range(lax.axis_size(axis))])


def head_attend(queries, keys_all, values_all, live_keys):
    scores = jnp.einsum(
        "sd,kd->sk", queries, keys_all, preferred_element_type=jnp.float32
    ) * HD ** (-0.5)
    scores = jnp.where(live_keys[None, :], scores, -jnp.inf)
    peak_score = jnp.max(scores, axis=1, keepdims=True)
    raw_weights = jnp.exp(scores - peak_score)
    row_total = jnp.sum(raw_weights, axis=1, keepdims=True)
    weights = raw_weights.astype(jnp.bfloat16)
    return (
        jnp.einsum("sk,kd->sd", weights, values_all, preferred_element_type=jnp.float32)
        / row_total
    )


def radix4_digits(n):
    assert n == 64
    return [2, 0, 4]


def shards(
    query,
    keys,
    values,
    hidden,
    latent,
    deal,
    lengths,
    w_out,
    attn_gate,
    modulation,
    w_final,
    guide,
    step_size,
):
    nseq = lax.axis_size("seq")
    group_id = lax.axis_index("grp")
    branch = lax.axis_index("cfg")
    partner = jnp.bitwise_xor(group_id, 1)
    own_lengths = lax.dynamic_index_in_dim(lengths, group_id, 0, keepdims=False)
    pair_lengths = lax.dynamic_index_in_dim(lengths, partner, 0, keepdims=False)
    item_ids = lax.dynamic_index_in_dim(deal, group_id, 0, keepdims=False)
    local_query = query[0, 0]
    resident_key_rows = keys[0, 0]
    local_values = values[0, 0]
    shard_rows = resident_key_rows.shape[1]
    slot_total = nseq * shard_rows
    far_keys, far_values = from_partner((resident_key_rows[1], local_values[1]), "grp", 0)

    def to_heads(x):
        n = x.shape[0]
        x = x.reshape(n, shard_rows, HEADS, HD).transpose(2, 0, 1, 3)
        return jnp.pad(x, ((0, nseq - HEADS), (0, 0), (0, 0), (0, 0)))

    block_rows = w_out.shape[0]
    col_width = D // nseq
    w_parts = w_out.reshape(block_rows, nseq, col_width).transpose(1, 0, 2)
    packed = jnp.concatenate(
        [
            to_heads(local_query),
            to_heads(jnp.concatenate([resident_key_rows, far_keys[None]], 0)),
            to_heads(jnp.concatenate([local_values, far_values[None]], 0)),
        ],
        axis=1,
    )
    head_width = packed.shape[1] * shard_rows * HD
    joint = jnp.concatenate(
        [packed.reshape(nseq, head_width), w_parts.reshape(nseq, block_rows * col_width)], 1
    )
    joint = lax.all_to_all(joint, "seq", 0, 0, tiled=True)
    head_rows = joint[:, :head_width].reshape(nseq, 8, shard_rows, HD)
    head_rows = head_rows.transpose(1, 0, 2, 3).reshape(8, slot_total, HD)
    head_q, head_k, head_v = head_rows[0:2], head_rows[2:5], head_rows[5:8]
    slot_ids = jnp.arange(slot_total)
    live_home = slot_ids < own_lengths[0]
    live_own = slot_ids < own_lengths[1]
    live_pair = slot_ids < pair_lengths[1]
    home_out = head_attend(head_q[0], head_k[0], head_v[0], live_home)
    shared_out = head_attend(
        head_q[1],
        jnp.concatenate([head_k[1], head_k[2]], 0),
        jnp.concatenate([head_v[1], head_v[2]], 0),
        jnp.concatenate([live_own, live_pair], 0),
    )
    head_attn = jnp.stack([home_out, shared_out]).astype(jnp.bfloat16)

    w_half = joint[:, head_width:].reshape(nseq * block_rows, col_width)
    w_other = from_partner(w_half, "cfg", 0)
    w_cols = jnp.where(
        branch == 0,
        jnp.concatenate([w_half, w_other], 0),
        jnp.concatenate([w_other, w_half], 0),
    )

    me = lax.axis_index("seq")
    gathered = head_attn[None]
    masks = [0]
    for low_bit in radix4_digits(nseq):
        parts = [gathered]
        grown = list(masks)
        for digit in (1, 2, 3):
            shift = digit << low_bit
            parts.append(lax.ppermute(gathered, "seq", [(i, i ^ shift) for i in range(nseq)]))
            grown += [m ^ shift for m in masks]
        gathered = jnp.concatenate(parts, 0)
        masks = grown
    source_head = jnp.bitwise_xor(me, jnp.array(masks, jnp.int32))
    w_heads = jnp.pad(
        w_cols.reshape(HEADS, HD, col_width), ((0, nseq - HEADS), (0, 0), (0, 0))
    )
    w_ordered = jnp.take(w_heads, source_head, axis=0)
    projected_cols = jnp.einsum(
        "irsd,idc->rsc", gathered, w_ordered, preferred_element_type=jnp.float32
    ).reshape(2 * slot_total, col_width)
    projected_parts = projected_cols.reshape(2, nseq, shard_rows, col_width).transpose(1, 0, 2, 3)
    projected = lax.all_to_all(projected_parts, "seq", 0, 0, tiled=True)
    projected = projected.transpose(1, 2, 0, 3).reshape(2, shard_rows, D)

    item_count = guide.shape[0]
    indicator_mask = (jnp.arange(item_count)[None, :] == item_ids[:, None]).astype(jnp.float32)
    gate_now = jnp.einsum(
        "ri,id->rd", indicator_mask, attn_gate[0], precision=lax.Precision.HIGHEST
    )
    stream = hidden[0, 0].astype(jnp.float32) + gate_now[:, None, :] * projected
    row_mean = jnp.mean(stream, axis=2, keepdims=True)
    centred = stream - row_mean
    row_var = jnp.mean(centred * centred, axis=2, keepdims=True)
    normed = centred * lax.rsqrt(row_var + NORM_EPS)
    selected_entries = jnp.einsum(
        "ub,bkg->ukg", indicator_mask, modulation[0], precision=lax.Precision.HIGHEST
    )
    shaped = (
        normed * (1.0 + selected_entries[:, 1][:, None, :]) + selected_entries[:, 0][:, None, :]
    ).astype(jnp.bfloat16)
    velocity = jnp.einsum("rsd,dc->rsc", shaped, w_final, preferred_element_type=jnp.float32)
    row_slots = lax.axis_index("seq") * shard_rows + jnp.arange(shard_rows)
    live_rows = jnp.stack([row_slots < own_lengths[0], row_slots < own_lengths[1]])
    velocity = jnp.where(live_rows[:, :, None], velocity, jnp.float32(0.0))
    weight_now = jnp.sum(indicator_mask * guide[None, :], axis=1)[:, None, None]
    step_now = jnp.sum(indicator_mask * step_size[None, :], axis=1)[:, None, None]
    latent_part = latent[0]
    part_width = latent_part.shape[2]
    outgoing_velocity = lax.dynamic_slice_in_dim(velocity, (1 - branch) * part_width, part_width, 2)
    own_velocity = lax.dynamic_slice_in_dim(velocity, branch * part_width, part_width, 2)
    other_velocity = from_partner(outgoing_velocity, "cfg", 0)
    is_conditional = branch == 0
    cond_velocity = jnp.where(is_conditional, own_velocity, other_velocity)
    uncond_velocity = jnp.where(is_conditional, other_velocity, own_velocity)
    guided = uncond_velocity + weight_now * (cond_velocity - uncond_velocity)
    updated = latent_part - step_now * guided
    return updated[None]


def solution(mesh):
    placed = (
        P("cfg", "grp", None, "seq", None),
        P("cfg", "grp", None, "seq", None),
        P("cfg", "grp", None, "seq", None),
        P("cfg", "grp", None, "seq", None),
        P("grp", None, "seq", "cfg"),
        P(),
        P(),
        P(("cfg", "seq"), None),
        P("cfg", None, None),
        P("cfg", None, None, None),
        P(),
        P(),
        P(),
    )
    return jax.shard_map(
        shards, mesh=mesh, in_specs=placed, out_specs=P("grp", None, "seq", "cfg"), check_vma=False
    )
```

```python
import jax
import jax.numpy as jnp
from jax import lax
from jax.sharding import PartitionSpec as P

D = 2432
HEADS = 38
HD = 64


NORM_EPS = 1e-06


def from_partner(x, axis, apart):
    return lax.ppermute(x, axis, [(i, i ^ 1 << apart) for i in range(lax.axis_size(axis))])


def head_attend(queries, keys_all, values_all, live_keys):
    scores = jnp.einsum(
        "sd,kd->sk", queries, keys_all, preferred_element_type=jnp.float32
    ) * HD ** (-0.5)
    scores = jnp.where(live_keys[None, :], scores, -jnp.inf)
    peak_score = jnp.max(scores, axis=1, keepdims=True)
    raw_weights = jnp.exp(scores - peak_score)
    row_total = jnp.sum(raw_weights, axis=1, keepdims=True)
    weights = raw_weights.astype(jnp.bfloat16)
    return (
        jnp.einsum("sk,kd->sd", weights, values_all, preferred_element_type=jnp.float32)
        / row_total
    )


def plane_heads(n):
    assert n == 64
    return -(-HEADS // 4)


def head_placement(n):
    used = plane_heads(n)
    table = []
    for j in range(n):
        x, z = divmod(j, 16)
        head = x * used + z
        table.append(head if z < used and head < HEADS else HEADS)
    return table


def shards(
    query,
    keys,
    values,
    hidden,
    latent,
    deal,
    lengths,
    w_out,
    attn_gate,
    modulation,
    w_final,
    guide,
    step_size,
):
    nseq = lax.axis_size("seq")
    group_id = lax.axis_index("grp")
    branch = lax.axis_index("cfg")
    partner = jnp.bitwise_xor(group_id, 1)
    own_lengths = lax.dynamic_index_in_dim(lengths, group_id, 0, keepdims=False)
    pair_lengths = lax.dynamic_index_in_dim(lengths, partner, 0, keepdims=False)
    item_ids = lax.dynamic_index_in_dim(deal, group_id, 0, keepdims=False)
    local_query = query[0, 0]
    resident_key_rows = keys[0, 0]
    local_values = values[0, 0]
    shard_rows = resident_key_rows.shape[1]
    slot_total = nseq * shard_rows
    far_keys, far_values = from_partner((resident_key_rows[1], local_values[1]), "grp", 0)

    head_table = head_placement(nseq)

    def to_heads(x):
        n = x.shape[0]
        x = x.reshape(n, shard_rows, HEADS, HD).transpose(2, 0, 1, 3)
        x = jnp.pad(x, ((0, 1), (0, 0), (0, 0), (0, 0)))
        return jnp.take(x, jnp.array(head_table, jnp.int32), axis=0)

    block_rows = w_out.shape[0]
    col_width = D // nseq
    w_parts = w_out.reshape(block_rows, nseq, col_width).transpose(1, 0, 2)
    packed = jnp.concatenate(
        [
            to_heads(local_query),
            to_heads(jnp.concatenate([resident_key_rows, far_keys[None]], 0)),
            to_heads(jnp.concatenate([local_values, far_values[None]], 0)),
        ],
        axis=1,
    )
    head_width = packed.shape[1] * shard_rows * HD
    joint = jnp.concatenate(
        [packed.reshape(nseq, head_width), w_parts.reshape(nseq, block_rows * col_width)], 1
    )
    joint = lax.all_to_all(joint, "seq", 0, 0, tiled=True)
    head_rows = joint[:, :head_width].reshape(nseq, 8, shard_rows, HD)
    head_rows = head_rows.transpose(1, 0, 2, 3).reshape(8, slot_total, HD)
    head_q, head_k, head_v = head_rows[0:2], head_rows[2:5], head_rows[5:8]
    slot_ids = jnp.arange(slot_total)
    live_home = slot_ids < own_lengths[0]
    live_own = slot_ids < own_lengths[1]
    live_pair = slot_ids < pair_lengths[1]
    home_out = head_attend(head_q[0], head_k[0], head_v[0], live_home)
    shared_out = head_attend(
        head_q[1],
        jnp.concatenate([head_k[1], head_k[2]], 0),
        jnp.concatenate([head_v[1], head_v[2]], 0),
        jnp.concatenate([live_own, live_pair], 0),
    )
    head_attn = jnp.stack([home_out, shared_out]).astype(jnp.bfloat16)

    w_half = joint[:, head_width:].reshape(nseq * block_rows, col_width)
    w_other = from_partner(w_half, "cfg", 0)
    w_cols = jnp.where(
        branch == 0,
        jnp.concatenate([w_half, w_other], 0),
        jnp.concatenate([w_other, w_half], 0),
    )

    me = lax.axis_index("seq")
    gathered = head_attn[None]
    masks = [0]
    for low_bit in (2, 0):
        parts = [gathered]
        grown = list(masks)
        for digit in (1, 2, 3):
            shift = digit << low_bit
            parts.append(lax.ppermute(gathered, "seq", [(i, i ^ shift) for i in range(nseq)]))
            grown += [m ^ shift for m in masks]
        gathered = jnp.concatenate(parts, 0)
        masks = grown
    plane = len(masks)
    inverse = [masks.index(z) for z in range(plane)]
    my_z = me % plane
    my_x = me // plane
    by_z = jnp.take(gathered, jnp.take(jnp.array(inverse, jnp.int32), jnp.bitwise_xor(my_z, jnp.arange(plane))), axis=0)
    used = plane_heads(nseq)
    outgoing = by_z[:used]
    parts = [by_z]
    sources = [my_x * plane + jnp.arange(plane)]
    for digit in (1, 2, 3):
        shift = digit * plane
        parts.append(lax.ppermute(outgoing, "seq", [(i, i ^ shift) for i in range(nseq)]))
        sources.append(jnp.bitwise_xor(my_x, digit) * plane + jnp.arange(used))
    gathered = jnp.concatenate(parts, 0)
    source_head = jnp.take(jnp.array(head_table, jnp.int32), jnp.concatenate(sources))
    w_heads = jnp.pad(w_cols.reshape(HEADS, HD, col_width), ((0, 1), (0, 0), (0, 0)))
    w_ordered = jnp.take(w_heads, source_head, axis=0)
    projected_cols = jnp.einsum(
        "irsd,idc->rsc", gathered, w_ordered, preferred_element_type=jnp.float32
    ).reshape(2 * slot_total, col_width)
    projected_parts = projected_cols.reshape(2, nseq, shard_rows, col_width).transpose(1, 0, 2, 3)
    projected = lax.all_to_all(projected_parts, "seq", 0, 0, tiled=True)
    projected = projected.transpose(1, 2, 0, 3).reshape(2, shard_rows, D)

    item_count = guide.shape[0]
    indicator_mask = (jnp.arange(item_count)[None, :] == item_ids[:, None]).astype(jnp.float32)
    gate_now = jnp.einsum(
        "ri,id->rd", indicator_mask, attn_gate[0], precision=lax.Precision.HIGHEST
    )
    stream = hidden[0, 0].astype(jnp.float32) + gate_now[:, None, :] * projected
    row_mean = jnp.mean(stream, axis=2, keepdims=True)
    centred = stream - row_mean
    row_var = jnp.mean(centred * centred, axis=2, keepdims=True)
    normed = centred * lax.rsqrt(row_var + NORM_EPS)
    selected_entries = jnp.einsum(
        "ub,bkg->ukg", indicator_mask, modulation[0], precision=lax.Precision.HIGHEST
    )
    shaped = (
        normed * (1.0 + selected_entries[:, 1][:, None, :]) + selected_entries[:, 0][:, None, :]
    ).astype(jnp.bfloat16)
    velocity = jnp.einsum("rsd,dc->rsc", shaped, w_final, preferred_element_type=jnp.float32)
    row_slots = lax.axis_index("seq") * shard_rows + jnp.arange(shard_rows)
    live_rows = jnp.stack([row_slots < own_lengths[0], row_slots < own_lengths[1]])
    velocity = jnp.where(live_rows[:, :, None], velocity, jnp.float32(0.0))
    weight_now = jnp.sum(indicator_mask * guide[None, :], axis=1)[:, None, None]
    step_now = jnp.sum(indicator_mask * step_size[None, :], axis=1)[:, None, None]
    latent_part = latent[0]
    part_width = latent_part.shape[2]
    outgoing_velocity = lax.dynamic_slice_in_dim(velocity, (1 - branch) * part_width, part_width, 2)
    own_velocity = lax.dynamic_slice_in_dim(velocity, branch * part_width, part_width, 2)
    other_velocity = from_partner(outgoing_velocity, "cfg", 0)
    is_conditional = branch == 0
    cond_velocity = jnp.where(is_conditional, own_velocity, other_velocity)
    uncond_velocity = jnp.where(is_conditional, other_velocity, own_velocity)
    guided = uncond_velocity + weight_now * (cond_velocity - uncond_velocity)
    updated = latent_part - step_now * guided
    return updated[None]


def solution(mesh):
    placed = (
        P("cfg", "grp", None, "seq", None),
        P("cfg", "grp", None, "seq", None),
        P("cfg", "grp", None, "seq", None),
        P("cfg", "grp", None, "seq", None),
        P("grp", None, "seq", "cfg"),
        P(),
        P(),
        P(("cfg", "seq"), None),
        P("cfg", None, None),
        P("cfg", None, None, None),
        P(),
        P(),
        P(),
    )
    return jax.shard_map(
        shards, mesh=mesh, in_specs=placed, out_specs=P("grp", None, "seq", "cfg"), check_vma=False
    )
```

```python
import jax
import jax.numpy as jnp
from jax import lax
from jax.sharding import PartitionSpec as P

D = 2432
HEADS = 38
HD = 64


NORM_EPS = 1e-06


def from_partner(x, axis, apart):
    return lax.ppermute(x, axis, [(i, i ^ 1 << apart) for i in range(lax.axis_size(axis))])


def head_attend(queries, keys_all, values_all, live_keys):
    scores = jnp.einsum(
        "sd,kd->sk", queries, keys_all, preferred_element_type=jnp.float32
    ) * HD ** (-0.5)
    scores = jnp.where(live_keys[None, :], scores, -jnp.inf)
    peak_score = jnp.max(scores, axis=1, keepdims=True)
    raw_weights = jnp.exp(scores - peak_score)
    row_total = jnp.sum(raw_weights, axis=1, keepdims=True)
    weights = raw_weights.astype(jnp.bfloat16)
    return (
        jnp.einsum("sk,kd->sd", weights, values_all, preferred_element_type=jnp.float32)
        / row_total
    )


def projection_split(n):
    regions, chunks = [], []
    for j in range(n):
        x, z = divmod(j, 16)
        regions.append(x % 2)
        chunks.append((x // 2) * 16 + z)
    return regions, chunks


def owner_of(region_of, chunk_of, region, chunk):
    return [j for j in range(len(region_of)) if region_of[j] == region and chunk_of[j] == chunk][0]


def plane_heads(n):
    assert n == 64
    return -(-HEADS // 4)


def head_placement(n):
    used = plane_heads(n)
    table = []
    for j in range(n):
        x, z = divmod(j, 16)
        head = x * used + z
        table.append(head if z < used and head < HEADS else HEADS)
    return table


def shards(
    query,
    keys,
    values,
    hidden,
    latent,
    deal,
    lengths,
    w_out,
    attn_gate,
    modulation,
    w_final,
    guide,
    step_size,
):
    nseq = lax.axis_size("seq")
    group_id = lax.axis_index("grp")
    branch = lax.axis_index("cfg")
    partner = jnp.bitwise_xor(group_id, 1)
    own_lengths = lax.dynamic_index_in_dim(lengths, group_id, 0, keepdims=False)
    pair_lengths = lax.dynamic_index_in_dim(lengths, partner, 0, keepdims=False)
    item_ids = lax.dynamic_index_in_dim(deal, group_id, 0, keepdims=False)
    local_query = query[0, 0]
    resident_key_rows = keys[0, 0]
    local_values = values[0, 0]
    shard_rows = resident_key_rows.shape[1]
    slot_total = nseq * shard_rows
    far_keys, far_values = from_partner((resident_key_rows[1], local_values[1]), "grp", 0)

    head_table = head_placement(nseq)

    def to_heads(x):
        n = x.shape[0]
        x = x.reshape(n, shard_rows, HEADS, HD).transpose(2, 0, 1, 3)
        x = jnp.pad(x, ((0, 1), (0, 0), (0, 0), (0, 0)))
        return jnp.take(x, jnp.array(head_table, jnp.int32), axis=0)

    block_rows = w_out.shape[0]
    region_of, chunk_of = projection_split(nseq)
    chunks = max(chunk_of) + 1
    col_width = D // chunks
    w_parts = w_out.reshape(block_rows, chunks, col_width).transpose(1, 0, 2)
    w_parts = jnp.take(w_parts, jnp.array(chunk_of, jnp.int32), axis=0)
    packed = jnp.concatenate(
        [
            to_heads(local_query),
            to_heads(jnp.concatenate([resident_key_rows, far_keys[None]], 0)),
            to_heads(jnp.concatenate([local_values, far_values[None]], 0)),
        ],
        axis=1,
    )
    head_width = packed.shape[1] * shard_rows * HD
    joint = jnp.concatenate(
        [packed.reshape(nseq, head_width), w_parts.reshape(nseq, block_rows * col_width)], 1
    )
    joint = lax.all_to_all(joint, "seq", 0, 0, tiled=True)
    head_rows = joint[:, :head_width].reshape(nseq, 8, shard_rows, HD)
    head_rows = head_rows.transpose(1, 0, 2, 3).reshape(8, slot_total, HD)
    head_q, head_k, head_v = head_rows[0:2], head_rows[2:5], head_rows[5:8]
    slot_ids = jnp.arange(slot_total)
    live_home = slot_ids < own_lengths[0]
    live_own = slot_ids < own_lengths[1]
    live_pair = slot_ids < pair_lengths[1]
    home_out = head_attend(head_q[0], head_k[0], head_v[0], live_home)
    shared_out = head_attend(
        head_q[1],
        jnp.concatenate([head_k[1], head_k[2]], 0),
        jnp.concatenate([head_v[1], head_v[2]], 0),
        jnp.concatenate([live_own, live_pair], 0),
    )
    head_attn = jnp.stack([home_out, shared_out]).astype(jnp.bfloat16)

    w_half = joint[:, head_width:].reshape(nseq * block_rows, col_width)
    w_other = from_partner(w_half, "cfg", 0)
    w_cols = jnp.where(
        branch == 0,
        jnp.concatenate([w_half, w_other], 0),
        jnp.concatenate([w_other, w_half], 0),
    )

    me = lax.axis_index("seq")
    gathered = head_attn[None]
    masks = [0]
    for low_bit in (2, 0):
        parts = [gathered]
        grown = list(masks)
        for digit in (1, 2, 3):
            shift = digit << low_bit
            parts.append(lax.ppermute(gathered, "seq", [(i, i ^ shift) for i in range(nseq)]))
            grown += [m ^ shift for m in masks]
        gathered = jnp.concatenate(parts, 0)
        masks = grown
    plane = len(masks)
    inverse = [masks.index(z) for z in range(plane)]
    my_z = me % plane
    my_x = me // plane
    by_z = jnp.take(gathered, jnp.take(jnp.array(inverse, jnp.int32), jnp.bitwise_xor(my_z, jnp.arange(plane))), axis=0)
    used = plane_heads(nseq)
    my_region = my_x % 2
    parts = [lax.dynamic_index_in_dim(by_z, my_region, 1, keepdims=False)]
    sources = [my_x * plane + jnp.arange(plane)]
    for digit in (1, 2, 3):
        shift = digit * plane
        outgoing = lax.dynamic_index_in_dim(by_z[:used], (my_x ^ digit) % 2, 1, keepdims=False)
        parts.append(lax.ppermute(outgoing, "seq", [(i, i ^ shift) for i in range(nseq)]))
        sources.append(jnp.bitwise_xor(my_x, digit) * plane + jnp.arange(used))
    gathered = jnp.concatenate(parts, 0)
    source_head = jnp.take(jnp.array(head_table, jnp.int32), jnp.concatenate(sources))
    w_heads = jnp.pad(w_cols.reshape(HEADS, HD, col_width), ((0, 1), (0, 0), (0, 0)))
    w_ordered = jnp.take(w_heads, source_head, axis=0)
    projected_cols = jnp.einsum(
        "isd,idc->sc", gathered, w_ordered, preferred_element_type=jnp.float32
    )
    projected_parts = projected_cols.reshape(nseq, shard_rows, col_width)
    received = lax.all_to_all(projected_parts, "seq", 0, 0, tiled=True)
    by_region = []
    for region in range(2):
        owners = [owner_of(region_of, chunk_of, region, c) for c in range(chunks)]
        picked = jnp.take(received, jnp.array(owners, jnp.int32), axis=0)
        by_region.append(picked.transpose(1, 0, 2).reshape(shard_rows, D))
    projected = jnp.stack(by_region)

    item_count = guide.shape[0]
    indicator_mask = (jnp.arange(item_count)[None, :] == item_ids[:, None]).astype(jnp.float32)
    gate_now = jnp.einsum(
        "ri,id->rd", indicator_mask, attn_gate[0], precision=lax.Precision.HIGHEST
    )
    stream = hidden[0, 0].astype(jnp.float32) + gate_now[:, None, :] * projected
    row_mean = jnp.mean(stream, axis=2, keepdims=True)
    centred = stream - row_mean
    row_var = jnp.mean(centred * centred, axis=2, keepdims=True)
    normed = centred * lax.rsqrt(row_var + NORM_EPS)
    selected_entries = jnp.einsum(
        "ub,bkg->ukg", indicator_mask, modulation[0], precision=lax.Precision.HIGHEST
    )
    shaped = (
        normed * (1.0 + selected_entries[:, 1][:, None, :]) + selected_entries[:, 0][:, None, :]
    ).astype(jnp.bfloat16)
    velocity = jnp.einsum("rsd,dc->rsc", shaped, w_final, preferred_element_type=jnp.float32)
    row_slots = lax.axis_index("seq") * shard_rows + jnp.arange(shard_rows)
    live_rows = jnp.stack([row_slots < own_lengths[0], row_slots < own_lengths[1]])
    velocity = jnp.where(live_rows[:, :, None], velocity, jnp.float32(0.0))
    weight_now = jnp.sum(indicator_mask * guide[None, :], axis=1)[:, None, None]
    step_now = jnp.sum(indicator_mask * step_size[None, :], axis=1)[:, None, None]
    latent_part = latent[0]
    part_width = latent_part.shape[2]
    outgoing_velocity = lax.dynamic_slice_in_dim(velocity, (1 - branch) * part_width, part_width, 2)
    own_velocity = lax.dynamic_slice_in_dim(velocity, branch * part_width, part_width, 2)
    other_velocity = from_partner(outgoing_velocity, "cfg", 0)
    is_conditional = branch == 0
    cond_velocity = jnp.where(is_conditional, own_velocity, other_velocity)
    uncond_velocity = jnp.where(is_conditional, other_velocity, own_velocity)
    guided = uncond_velocity + weight_now * (cond_velocity - uncond_velocity)
    updated = latent_part - step_now * guided
    return updated[None]


def solution(mesh):
    placed = (
        P("cfg", "grp", None, "seq", None),
        P("cfg", "grp", None, "seq", None),
        P("cfg", "grp", None, "seq", None),
        P("cfg", "grp", None, "seq", None),
        P("grp", None, "seq", "cfg"),
        P(),
        P(),
        P(("cfg", "seq"), None),
        P("cfg", None, None),
        P("cfg", None, None, None),
        P(),
        P(),
        P(),
    )
    return jax.shard_map(
        shards, mesh=mesh, in_specs=placed, out_specs=P("grp", None, "seq", "cfg"), check_vma=False
    )
```

```python
import jax
import jax.numpy as jnp
from jax import lax
from jax.sharding import PartitionSpec as P

D = 2432
HEADS = 38
HD = 64


NORM_EPS = 1e-06


def from_partner(x, axis, apart):
    return lax.ppermute(x, axis, [(i, i ^ 1 << apart) for i in range(lax.axis_size(axis))])


def head_attend(queries, keys_all, values_all, live_keys):
    scores = jnp.einsum(
        "sd,kd->sk", queries, keys_all, preferred_element_type=jnp.float32
    ) * HD ** (-0.5)
    scores = jnp.where(live_keys[None, :], scores, -jnp.inf)
    peak_score = jnp.max(scores, axis=1, keepdims=True)
    raw_weights = jnp.exp(scores - peak_score)
    row_total = jnp.sum(raw_weights, axis=1, keepdims=True)
    weights = raw_weights.astype(jnp.bfloat16)
    return (
        jnp.einsum("sk,kd->sd", weights, values_all, preferred_element_type=jnp.float32)
        / row_total
    )


def projection_split(n):
    regions, chunks = [], []
    for j in range(n):
        x, z = divmod(j, 16)
        regions.append(x % 2)
        chunks.append((x // 2) * 16 + z)
    return regions, chunks


def owner_of(region_of, chunk_of, region, chunk):
    return [j for j in range(len(region_of)) if region_of[j] == region and chunk_of[j] == chunk][0]


def plane_heads(n):
    assert n == 64
    return -(-HEADS // 4)


def head_placement(n):
    used = plane_heads(n)
    table = []
    for j in range(n):
        x, z = divmod(j, 16)
        head = x * used + z
        table.append(head if z < used and head < HEADS else HEADS)
    return table


def shards(
    query,
    keys,
    values,
    hidden,
    latent,
    deal,
    lengths,
    w_out,
    attn_gate,
    modulation,
    w_final,
    guide,
    step_size,
):
    nseq = lax.axis_size("seq")
    group_id = lax.axis_index("grp")
    branch = lax.axis_index("cfg")
    partner = jnp.bitwise_xor(group_id, 1)
    own_lengths = lax.dynamic_index_in_dim(lengths, group_id, 0, keepdims=False)
    pair_lengths = lax.dynamic_index_in_dim(lengths, partner, 0, keepdims=False)
    item_ids = lax.dynamic_index_in_dim(deal, group_id, 0, keepdims=False)
    local_query = query[0, 0]
    resident_key_rows = keys[0, 0]
    local_values = values[0, 0]
    shard_rows = resident_key_rows.shape[1]
    slot_total = nseq * shard_rows
    far_keys, far_values = from_partner((resident_key_rows[1], local_values[1]), "grp", 0)

    head_table = head_placement(nseq)

    used = plane_heads(nseq)
    planes = nseq // 16

    def to_heads(x):
        n = x.shape[0]
        x = x.reshape(n, shard_rows, HEADS, HD).transpose(2, 0, 1, 3)
        x = jnp.pad(x, ((0, planes * used - HEADS), (0, 0), (0, 0), (0, 0)))
        x = x.reshape(planes, used, n, shard_rows, HD)
        x = jnp.pad(x, ((0, 0), (0, 16 - used), (0, 0), (0, 0), (0, 0)))
        return x.reshape(nseq, n, shard_rows, HD)

    region_of, chunk_of = projection_split(nseq)
    chunks = max(chunk_of) + 1
    block_rows = w_out.shape[0]
    col_width = D // chunks
    w_parts = w_out.reshape(block_rows, chunks, col_width).transpose(1, 0, 2)
    w_parts = w_parts.reshape(planes // 2, 1, 16, block_rows, col_width)
    w_parts = jnp.broadcast_to(w_parts, (planes // 2, 2, 16, block_rows, col_width))
    w_parts = w_parts.reshape(nseq, block_rows, col_width)
    packed = to_heads(
        jnp.concatenate(
            [local_query, resident_key_rows, far_keys[None], local_values, far_values[None]], 0
        )
    )
    head_width = packed.shape[1] * shard_rows * HD
    joint = jnp.concatenate(
        [packed.reshape(nseq, head_width), w_parts.reshape(nseq, block_rows * col_width)], 1
    )
    joint = lax.all_to_all(joint, "seq", 0, 0, tiled=True)
    head_rows = joint[:, :head_width].reshape(nseq, 8, shard_rows, HD)
    head_rows = head_rows.transpose(1, 0, 2, 3).reshape(8, slot_total, HD)
    head_q, head_k, head_v = head_rows[0:2], head_rows[2:5], head_rows[5:8]
    slot_ids = jnp.arange(slot_total)
    live_home = slot_ids < own_lengths[0]
    live_own = slot_ids < own_lengths[1]
    live_pair = slot_ids < pair_lengths[1]
    home_out = head_attend(head_q[0], head_k[0], head_v[0], live_home)
    shared_out = head_attend(
        head_q[1],
        jnp.concatenate([head_k[1], head_k[2]], 0),
        jnp.concatenate([head_v[1], head_v[2]], 0),
        jnp.concatenate([live_own, live_pair], 0),
    )
    head_attn = jnp.stack([home_out, shared_out]).astype(jnp.bfloat16)

    w_half = joint[:, head_width:].reshape(nseq * block_rows, col_width)
    w_other = from_partner(w_half, "cfg", 0)
    w_cols = jnp.where(
        branch == 0,
        jnp.concatenate([w_half, w_other], 0),
        jnp.concatenate([w_other, w_half], 0),
    )

    me = lax.axis_index("seq")
    gathered = head_attn[None]
    masks = [0]
    for low_bit in (2, 0):
        parts = [gathered]
        grown = list(masks)
        for digit in (1, 2, 3):
            shift = digit << low_bit
            parts.append(lax.ppermute(gathered, "seq", [(i, i ^ shift) for i in range(nseq)]))
            grown += [m ^ shift for m in masks]
        gathered = jnp.concatenate(parts, 0)
        masks = grown
    plane = len(masks)
    inverse = [masks.index(z) for z in range(plane)]
    my_z = me % plane
    my_x = me // plane
    by_z = jnp.take(gathered, jnp.take(jnp.array(inverse, jnp.int32), jnp.bitwise_xor(my_z, jnp.arange(plane))), axis=0)
    my_region = my_x % 2
    parts = [lax.dynamic_index_in_dim(by_z, my_region, 1, keepdims=False)]
    sources = [my_x * plane + jnp.arange(plane)]
    for digit in (1, 2, 3):
        shift = digit * plane
        outgoing = lax.dynamic_index_in_dim(by_z[:used], (my_x ^ digit) % 2, 1, keepdims=False)
        parts.append(lax.ppermute(outgoing, "seq", [(i, i ^ shift) for i in range(nseq)]))
        sources.append(jnp.bitwise_xor(my_x, digit) * plane + jnp.arange(used))
    gathered = jnp.concatenate(parts, 0)
    source_head = jnp.take(jnp.array(head_table, jnp.int32), jnp.concatenate(sources))
    w_heads = jnp.pad(w_cols.reshape(HEADS, HD, col_width), ((0, 1), (0, 0), (0, 0)))
    w_ordered = jnp.take(w_heads, source_head, axis=0)
    projected_cols = jnp.einsum(
        "isd,idc->sc", gathered, w_ordered, preferred_element_type=jnp.float32
    )
    projected_parts = projected_cols.reshape(nseq, shard_rows, col_width)
    received = lax.all_to_all(projected_parts, "seq", 0, 0, tiled=True)
    by_region = []
    for region in range(2):
        owners = [owner_of(region_of, chunk_of, region, c) for c in range(chunks)]
        picked = jnp.take(received, jnp.array(owners, jnp.int32), axis=0)
        by_region.append(picked.transpose(1, 0, 2).reshape(shard_rows, D))
    projected = jnp.stack(by_region)

    item_count = guide.shape[0]
    indicator_mask = (jnp.arange(item_count)[None, :] == item_ids[:, None]).astype(jnp.float32)
    gate_now = jnp.einsum(
        "ri,id->rd", indicator_mask, attn_gate[0], precision=lax.Precision.HIGHEST
    )
    stream = hidden[0, 0].astype(jnp.float32) + gate_now[:, None, :] * projected
    row_mean = jnp.mean(stream, axis=2, keepdims=True)
    centred = stream - row_mean
    row_var = jnp.mean(centred * centred, axis=2, keepdims=True)
    normed = centred * lax.rsqrt(row_var + NORM_EPS)
    selected_entries = jnp.einsum(
        "ub,bkg->ukg", indicator_mask, modulation[0], precision=lax.Precision.HIGHEST
    )
    shaped = (
        normed * (1.0 + selected_entries[:, 1][:, None, :]) + selected_entries[:, 0][:, None, :]
    ).astype(jnp.bfloat16)
    velocity = jnp.einsum("rsd,dc->rsc", shaped, w_final, preferred_element_type=jnp.float32)
    row_slots = lax.axis_index("seq") * shard_rows + jnp.arange(shard_rows)
    live_rows = jnp.stack([row_slots < own_lengths[0], row_slots < own_lengths[1]])
    velocity = jnp.where(live_rows[:, :, None], velocity, jnp.float32(0.0))
    weight_now = jnp.sum(indicator_mask * guide[None, :], axis=1)[:, None, None]
    step_now = jnp.sum(indicator_mask * step_size[None, :], axis=1)[:, None, None]
    latent_part = latent[0]
    part_width = latent_part.shape[2]
    outgoing_velocity = lax.dynamic_slice_in_dim(velocity, (1 - branch) * part_width, part_width, 2)
    own_velocity = lax.dynamic_slice_in_dim(velocity, branch * part_width, part_width, 2)
    other_velocity = from_partner(outgoing_velocity, "cfg", 0)
    is_conditional = branch == 0
    cond_velocity = jnp.where(is_conditional, own_velocity, other_velocity)
    uncond_velocity = jnp.where(is_conditional, other_velocity, own_velocity)
    guided = uncond_velocity + weight_now * (cond_velocity - uncond_velocity)
    updated = latent_part - step_now * guided
    return updated[None]


def solution(mesh):
    placed = (
        P("cfg", "grp", None, "seq", None),
        P("cfg", "grp", None, "seq", None),
        P("cfg", "grp", None, "seq", None),
        P("cfg", "grp", None, "seq", None),
        P("grp", None, "seq", "cfg"),
        P(),
        P(),
        P(("cfg", "seq"), None),
        P("cfg", None, None),
        P("cfg", None, None, None),
        P(),
        P(),
        P(),
    )
    return jax.shard_map(
        shards, mesh=mesh, in_specs=placed, out_specs=P("grp", None, "seq", "cfg"), check_vma=False
    )
```

```python
import jax
import jax.numpy as jnp
from jax import lax
from jax.sharding import PartitionSpec as P

D = 2432
HEADS = 38
HD = 64


NORM_EPS = 1e-06


def from_partner(x, axis, apart):
    return lax.ppermute(x, axis, [(i, i ^ 1 << apart) for i in range(lax.axis_size(axis))])


def head_attend(queries, keys_all, values_all, live_keys):
    scores = jnp.einsum(
        "sd,kd->sk", queries, keys_all, preferred_element_type=jnp.float32
    ) * HD ** (-0.5)
    scores = jnp.where(live_keys[None, :], scores, -jnp.inf)
    peak_score = jnp.max(scores, axis=1, keepdims=True)
    raw_weights = jnp.exp(scores - peak_score)
    row_total = jnp.sum(raw_weights, axis=1, keepdims=True)
    weights = raw_weights.astype(jnp.bfloat16)
    return (
        jnp.einsum("sk,kd->sd", weights, values_all, preferred_element_type=jnp.float32)
        / row_total
    )


def projection_split(n):
    regions, chunks = [], []
    for j in range(n):
        x, z = divmod(j, 16)
        regions.append(x % 2)
        chunks.append((x // 2) * 16 + z)
    return regions, chunks


def owner_of(region_of, chunk_of, region, chunk):
    return [j for j in range(len(region_of)) if region_of[j] == region and chunk_of[j] == chunk][0]


def plane_heads(n):
    assert n == 64
    return -(-HEADS // 4)


def head_placement(n):
    used = plane_heads(n)
    table = []
    for j in range(n):
        x, z = divmod(j, 16)
        head = x * used + z
        table.append(head if z < used and head < HEADS else HEADS)
    return table


def shards(
    query,
    keys,
    values,
    hidden,
    latent,
    deal,
    lengths,
    w_out,
    attn_gate,
    modulation,
    w_final,
    guide,
    step_size,
):
    nseq = lax.axis_size("seq")
    group_id = lax.axis_index("grp")
    branch = lax.axis_index("cfg")
    partner = jnp.bitwise_xor(group_id, 1)
    own_lengths = lax.dynamic_index_in_dim(lengths, group_id, 0, keepdims=False)
    pair_lengths = lax.dynamic_index_in_dim(lengths, partner, 0, keepdims=False)
    item_ids = lax.dynamic_index_in_dim(deal, group_id, 0, keepdims=False)
    local_query = query[0, 0]
    resident_key_rows = keys[0, 0]
    local_values = values[0, 0]
    shard_rows = resident_key_rows.shape[1]
    slot_total = nseq * shard_rows
    far_keys, far_values = from_partner((resident_key_rows[1], local_values[1]), "grp", 0)

    head_table = head_placement(nseq)

    used = plane_heads(nseq)
    planes = nseq // 16

    def to_heads(x):
        n = x.shape[0]
        x = x.reshape(n, shard_rows, HEADS, HD).transpose(2, 0, 1, 3)
        x = jnp.pad(x, ((0, planes * used - HEADS), (0, 0), (0, 0), (0, 0)))
        x = x.reshape(planes, used, n, shard_rows, HD)
        x = jnp.pad(x, ((0, 0), (0, 16 - used), (0, 0), (0, 0), (0, 0)))
        return x.reshape(nseq, n, shard_rows, HD)

    region_of, chunk_of = projection_split(nseq)
    chunks = max(chunk_of) + 1
    block_rows = w_out.shape[0]
    col_width = D // chunks
    w_parts = w_out.reshape(block_rows, chunks, col_width).transpose(1, 0, 2)
    w_parts = w_parts.reshape(planes // 2, 1, 16, block_rows, col_width)
    w_parts = jnp.broadcast_to(w_parts, (planes // 2, 2, 16, block_rows, col_width))
    w_parts = w_parts.reshape(nseq, block_rows, col_width)
    packed = to_heads(
        jnp.concatenate(
            [local_query, resident_key_rows, far_keys[None], local_values, far_values[None]], 0
        )
    )
    head_rows = lax.all_to_all(packed, "seq", 0, 0, tiled=True)
    head_rows = head_rows.transpose(1, 0, 2, 3).reshape(8, slot_total, HD)
    head_q, head_k, head_v = head_rows[0:2], head_rows[2:5], head_rows[5:8]
    slot_ids = jnp.arange(slot_total)
    live_home = slot_ids < own_lengths[0]
    live_own = slot_ids < own_lengths[1]
    live_pair = slot_ids < pair_lengths[1]
    home_out = head_attend(head_q[0], head_k[0], head_v[0], live_home)
    shared_out = head_attend(
        head_q[1],
        jnp.concatenate([head_k[1], head_k[2]], 0),
        jnp.concatenate([head_v[1], head_v[2]], 0),
        jnp.concatenate([live_own, live_pair], 0),
    )
    head_attn = jnp.stack([home_out, shared_out]).astype(jnp.bfloat16)

    w_parts, _ = lax.optimization_barrier((w_parts, head_attn))
    w_half = lax.all_to_all(w_parts, "seq", 0, 0, tiled=True).reshape(nseq * block_rows, col_width)
    w_other = from_partner(w_half, "cfg", 0)
    w_cols = jnp.where(
        branch == 0,
        jnp.concatenate([w_half, w_other], 0),
        jnp.concatenate([w_other, w_half], 0),
    )

    me = lax.axis_index("seq")
    gathered = head_attn[None]
    masks = [0]
    for low_bit in (2, 0):
        parts = [gathered]
        grown = list(masks)
        for digit in (1, 2, 3):
            shift = digit << low_bit
            parts.append(lax.ppermute(gathered, "seq", [(i, i ^ shift) for i in range(nseq)]))
            grown += [m ^ shift for m in masks]
        gathered = jnp.concatenate(parts, 0)
        masks = grown
    plane = len(masks)
    inverse = [masks.index(z) for z in range(plane)]
    my_z = me % plane
    my_x = me // plane
    by_z = jnp.take(gathered, jnp.take(jnp.array(inverse, jnp.int32), jnp.bitwise_xor(my_z, jnp.arange(plane))), axis=0)
    my_region = my_x % 2
    parts = [lax.dynamic_index_in_dim(by_z, my_region, 1, keepdims=False)]
    sources = [my_x * plane + jnp.arange(plane)]
    for digit in (1, 2, 3):
        shift = digit * plane
        outgoing = lax.dynamic_index_in_dim(by_z[:used], (my_x ^ digit) % 2, 1, keepdims=False)
        parts.append(lax.ppermute(outgoing, "seq", [(i, i ^ shift) for i in range(nseq)]))
        sources.append(jnp.bitwise_xor(my_x, digit) * plane + jnp.arange(used))
    gathered = jnp.concatenate(parts, 0)
    source_head = jnp.take(jnp.array(head_table, jnp.int32), jnp.concatenate(sources))
    w_heads = jnp.pad(w_cols.reshape(HEADS, HD, col_width), ((0, 1), (0, 0), (0, 0)))
    w_ordered = jnp.take(w_heads, source_head, axis=0)
    projected_cols = jnp.einsum(
        "isd,idc->sc", gathered, w_ordered, preferred_element_type=jnp.float32
    )
    projected_parts = projected_cols.reshape(nseq, shard_rows, col_width)
    received = lax.all_to_all(projected_parts, "seq", 0, 0, tiled=True)
    by_region = []
    for region in range(2):
        owners = [owner_of(region_of, chunk_of, region, c) for c in range(chunks)]
        picked = jnp.take(received, jnp.array(owners, jnp.int32), axis=0)
        by_region.append(picked.transpose(1, 0, 2).reshape(shard_rows, D))
    projected = jnp.stack(by_region)

    item_count = guide.shape[0]
    indicator_mask = (jnp.arange(item_count)[None, :] == item_ids[:, None]).astype(jnp.float32)
    gate_now = jnp.einsum(
        "ri,id->rd", indicator_mask, attn_gate[0], precision=lax.Precision.HIGHEST
    )
    stream = hidden[0, 0].astype(jnp.float32) + gate_now[:, None, :] * projected
    row_mean = jnp.mean(stream, axis=2, keepdims=True)
    centred = stream - row_mean
    row_var = jnp.mean(centred * centred, axis=2, keepdims=True)
    normed = centred * lax.rsqrt(row_var + NORM_EPS)
    selected_entries = jnp.einsum(
        "ub,bkg->ukg", indicator_mask, modulation[0], precision=lax.Precision.HIGHEST
    )
    shaped = (
        normed * (1.0 + selected_entries[:, 1][:, None, :]) + selected_entries[:, 0][:, None, :]
    ).astype(jnp.bfloat16)
    velocity = jnp.einsum("rsd,dc->rsc", shaped, w_final, preferred_element_type=jnp.float32)
    row_slots = lax.axis_index("seq") * shard_rows + jnp.arange(shard_rows)
    live_rows = jnp.stack([row_slots < own_lengths[0], row_slots < own_lengths[1]])
    velocity = jnp.where(live_rows[:, :, None], velocity, jnp.float32(0.0))
    weight_now = jnp.sum(indicator_mask * guide[None, :], axis=1)[:, None, None]
    step_now = jnp.sum(indicator_mask * step_size[None, :], axis=1)[:, None, None]
    latent_part = latent[0]
    part_width = latent_part.shape[2]
    outgoing_velocity = lax.dynamic_slice_in_dim(velocity, (1 - branch) * part_width, part_width, 2)
    own_velocity = lax.dynamic_slice_in_dim(velocity, branch * part_width, part_width, 2)
    other_velocity = from_partner(outgoing_velocity, "cfg", 0)
    is_conditional = branch == 0
    cond_velocity = jnp.where(is_conditional, own_velocity, other_velocity)
    uncond_velocity = jnp.where(is_conditional, other_velocity, own_velocity)
    guided = uncond_velocity + weight_now * (cond_velocity - uncond_velocity)
    updated = latent_part - step_now * guided
    return updated[None]


def solution(mesh):
    placed = (
        P("cfg", "grp", None, "seq", None),
        P("cfg", "grp", None, "seq", None),
        P("cfg", "grp", None, "seq", None),
        P("cfg", "grp", None, "seq", None),
        P("grp", None, "seq", "cfg"),
        P(),
        P(),
        P(("cfg", "seq"), None),
        P("cfg", None, None),
        P("cfg", None, None, None),
        P(),
        P(),
        P(),
    )
    return jax.shard_map(
        shards, mesh=mesh, in_specs=placed, out_specs=P("grp", None, "seq", "cfg"), check_vma=False
    )
```

```python
import jax
import jax.numpy as jnp
from jax import lax
from jax.sharding import PartitionSpec as P

D = 2432
HEADS = 38
HD = 64


NORM_EPS = 1e-06


def from_partner(x, axis, apart):
    return lax.ppermute(x, axis, [(i, i ^ 1 << apart) for i in range(lax.axis_size(axis))])


def head_attend(queries, keys_all, values_all, live_keys):
    scores = jnp.einsum(
        "sd,kd->sk", queries, keys_all, preferred_element_type=jnp.float32
    ) * HD ** (-0.5)
    scores = jnp.where(live_keys[None, :], scores, -jnp.inf)
    peak_score = jnp.max(scores, axis=1, keepdims=True)
    raw_weights = jnp.exp(scores - peak_score)
    row_total = jnp.sum(raw_weights, axis=1, keepdims=True)
    weights = raw_weights.astype(jnp.bfloat16)
    return (
        jnp.einsum("sk,kd->sd", weights, values_all, preferred_element_type=jnp.float32)
        / row_total
    )


def projection_split(n):
    regions, chunks = [], []
    for j in range(n):
        x, z = divmod(j, 16)
        regions.append(x % 2)
        chunks.append((x // 2) * 16 + z)
    return regions, chunks


def owner_of(region_of, chunk_of, region, chunk):
    return [j for j in range(len(region_of)) if region_of[j] == region and chunk_of[j] == chunk][0]


def plane_heads(n):
    assert n == 64
    return -(-HEADS // 4)


def head_placement(n):
    used = plane_heads(n)
    table = []
    for j in range(n):
        x, z = divmod(j, 16)
        head = x * used + z
        table.append(head if z < used and head < HEADS else HEADS)
    return table


def shards(
    query,
    keys,
    values,
    hidden,
    latent,
    deal,
    lengths,
    w_out,
    attn_gate,
    modulation,
    w_final,
    guide,
    step_size,
):
    nseq = lax.axis_size("seq")
    group_id = lax.axis_index("grp")
    branch = lax.axis_index("cfg")
    partner = jnp.bitwise_xor(group_id, 1)
    own_lengths = lax.dynamic_index_in_dim(lengths, group_id, 0, keepdims=False)
    pair_lengths = lax.dynamic_index_in_dim(lengths, partner, 0, keepdims=False)
    item_ids = lax.dynamic_index_in_dim(deal, group_id, 0, keepdims=False)
    local_query = query[0, 0]
    resident_key_rows = keys[0, 0]
    local_values = values[0, 0]
    shard_rows = resident_key_rows.shape[1]
    slot_total = nseq * shard_rows
    far_keys, far_values = from_partner(
        jnp.stack([resident_key_rows[1], local_values[1]]), "grp", 0
    )

    head_table = head_placement(nseq)

    used = plane_heads(nseq)
    planes = nseq // 16

    def to_heads(x):
        n = x.shape[0]
        x = x.reshape(n, shard_rows, HEADS, HD).transpose(2, 0, 1, 3)
        x = jnp.pad(x, ((0, planes * used - HEADS), (0, 0), (0, 0), (0, 0)))
        x = x.reshape(planes, used, n, shard_rows, HD)
        x = jnp.pad(x, ((0, 0), (0, 16 - used), (0, 0), (0, 0), (0, 0)))
        return x.reshape(nseq, n, shard_rows, HD)

    region_of, chunk_of = projection_split(nseq)
    chunks = max(chunk_of) + 1
    block_rows = w_out.shape[0]
    col_width = D // chunks
    w_parts = w_out.reshape(block_rows, chunks, col_width).transpose(1, 0, 2)
    w_parts = w_parts.reshape(planes // 2, 1, 16, block_rows, col_width)
    w_parts = jnp.broadcast_to(w_parts, (planes // 2, 2, 16, block_rows, col_width))
    w_parts = w_parts.reshape(nseq, block_rows, col_width)
    packed = to_heads(
        jnp.concatenate(
            [local_query, resident_key_rows, far_keys[None], local_values, far_values[None]], 0
        )
    )
    head_width = packed.shape[1] * shard_rows * HD
    joint = jnp.concatenate(
        [packed.reshape(nseq, head_width), w_parts.reshape(nseq, block_rows * col_width)], 1
    )
    joint = lax.all_to_all(joint, "seq", 0, 0, tiled=True)
    head_rows = joint[:, :head_width].reshape(nseq, 8, shard_rows, HD)
    head_rows = head_rows.transpose(1, 0, 2, 3).reshape(8, slot_total, HD)
    head_q, head_k, head_v = head_rows[0:2], head_rows[2:5], head_rows[5:8]
    slot_ids = jnp.arange(slot_total)
    live_home = slot_ids < own_lengths[0]
    live_own = slot_ids < own_lengths[1]
    live_pair = slot_ids < pair_lengths[1]
    home_out = head_attend(head_q[0], head_k[0], head_v[0], live_home)
    shared_out = head_attend(
        head_q[1],
        jnp.concatenate([head_k[1], head_k[2]], 0),
        jnp.concatenate([head_v[1], head_v[2]], 0),
        jnp.concatenate([live_own, live_pair], 0),
    )
    head_attn = jnp.stack([home_out, shared_out]).astype(jnp.bfloat16)

    w_half = joint[:, head_width:].reshape(nseq * block_rows, col_width)
    w_other = from_partner(w_half, "cfg", 0)
    w_cols = jnp.where(
        branch == 0,
        jnp.concatenate([w_half, w_other], 0),
        jnp.concatenate([w_other, w_half], 0),
    )

    me = lax.axis_index("seq")
    gathered = head_attn[None]
    masks = [0]
    for low_bit in (2, 0):
        parts = [gathered]
        grown = list(masks)
        for digit in (1, 2, 3):
            shift = digit << low_bit
            parts.append(lax.ppermute(gathered, "seq", [(i, i ^ shift) for i in range(nseq)]))
            grown += [m ^ shift for m in masks]
        gathered = jnp.concatenate(parts, 0)
        masks = grown
    plane = len(masks)
    inverse = [masks.index(z) for z in range(plane)]
    my_z = me % plane
    my_x = me // plane
    by_z = jnp.take(gathered, jnp.take(jnp.array(inverse, jnp.int32), jnp.bitwise_xor(my_z, jnp.arange(plane))), axis=0)
    my_region = my_x % 2
    parts = [lax.dynamic_index_in_dim(by_z, my_region, 1, keepdims=False)]
    sources = [my_x * plane + jnp.arange(plane)]
    for digit in (1, 2, 3):
        shift = digit * plane
        outgoing = lax.dynamic_index_in_dim(by_z[:used], (my_x ^ digit) % 2, 1, keepdims=False)
        parts.append(lax.ppermute(outgoing, "seq", [(i, i ^ shift) for i in range(nseq)]))
        sources.append(jnp.bitwise_xor(my_x, digit) * plane + jnp.arange(used))
    gathered = jnp.concatenate(parts, 0)
    source_head = jnp.take(jnp.array(head_table, jnp.int32), jnp.concatenate(sources))
    w_heads = jnp.pad(w_cols.reshape(HEADS, HD, col_width), ((0, 1), (0, 0), (0, 0)))
    w_ordered = jnp.take(w_heads, source_head, axis=0)
    projected_cols = jnp.einsum(
        "isd,idc->sc", gathered, w_ordered, preferred_element_type=jnp.float32
    )
    projected_parts = projected_cols.reshape(nseq, shard_rows, col_width)
    received = lax.all_to_all(projected_parts, "seq", 0, 0, tiled=True)
    by_region = []
    for region in range(2):
        owners = [owner_of(region_of, chunk_of, region, c) for c in range(chunks)]
        picked = jnp.take(received, jnp.array(owners, jnp.int32), axis=0)
        by_region.append(picked.transpose(1, 0, 2).reshape(shard_rows, D))
    projected = jnp.stack(by_region)

    item_count = guide.shape[0]
    indicator_mask = (jnp.arange(item_count)[None, :] == item_ids[:, None]).astype(jnp.float32)
    gate_now = jnp.einsum(
        "ri,id->rd", indicator_mask, attn_gate[0], precision=lax.Precision.HIGHEST
    )
    stream = hidden[0, 0].astype(jnp.float32) + gate_now[:, None, :] * projected
    row_mean = jnp.mean(stream, axis=2, keepdims=True)
    centred = stream - row_mean
    row_var = jnp.mean(centred * centred, axis=2, keepdims=True)
    normed = centred * lax.rsqrt(row_var + NORM_EPS)
    selected_entries = jnp.einsum(
        "ub,bkg->ukg", indicator_mask, modulation[0], precision=lax.Precision.HIGHEST
    )
    shaped = (
        normed * (1.0 + selected_entries[:, 1][:, None, :]) + selected_entries[:, 0][:, None, :]
    ).astype(jnp.bfloat16)
    velocity = jnp.einsum("rsd,dc->rsc", shaped, w_final, preferred_element_type=jnp.float32)
    row_slots = lax.axis_index("seq") * shard_rows + jnp.arange(shard_rows)
    live_rows = jnp.stack([row_slots < own_lengths[0], row_slots < own_lengths[1]])
    velocity = jnp.where(live_rows[:, :, None], velocity, jnp.float32(0.0))
    weight_now = jnp.sum(indicator_mask * guide[None, :], axis=1)[:, None, None]
    step_now = jnp.sum(indicator_mask * step_size[None, :], axis=1)[:, None, None]
    latent_part = latent[0]
    part_width = latent_part.shape[2]
    outgoing_velocity = lax.dynamic_slice_in_dim(velocity, (1 - branch) * part_width, part_width, 2)
    own_velocity = lax.dynamic_slice_in_dim(velocity, branch * part_width, part_width, 2)
    other_velocity = from_partner(outgoing_velocity, "cfg", 0)
    is_conditional = branch == 0
    cond_velocity = jnp.where(is_conditional, own_velocity, other_velocity)
    uncond_velocity = jnp.where(is_conditional, other_velocity, own_velocity)
    guided = uncond_velocity + weight_now * (cond_velocity - uncond_velocity)
    updated = latent_part - step_now * guided
    return updated[None]


def solution(mesh):
    placed = (
        P("cfg", "grp", None, "seq", None),
        P("cfg", "grp", None, "seq", None),
        P("cfg", "grp", None, "seq", None),
        P("cfg", "grp", None, "seq", None),
        P("grp", None, "seq", "cfg"),
        P(),
        P(),
        P(("cfg", "seq"), None),
        P("cfg", None, None),
        P("cfg", None, None, None),
        P(),
        P(),
        P(),
    )
    return jax.shard_map(
        shards, mesh=mesh, in_specs=placed, out_specs=P("grp", None, "seq", "cfg"), check_vma=False
    )
```

```python
import jax
import jax.numpy as jnp
from jax import lax
from jax.sharding import PartitionSpec as P

D = 2432
HEADS = 38
HD = 64


NORM_EPS = 1e-06


def from_partner(x, axis, apart):
    return lax.ppermute(x, axis, [(i, i ^ 1 << apart) for i in range(lax.axis_size(axis))])


def head_attend(queries, keys_all, values_all, live_keys):
    scores = jnp.einsum(
        "sd,kd->sk", queries, keys_all, preferred_element_type=jnp.float32
    ) * HD ** (-0.5)
    scores = jnp.where(live_keys[None, :], scores, -jnp.inf)
    peak_score = jnp.max(scores, axis=1, keepdims=True)
    raw_weights = jnp.exp(scores - peak_score)
    row_total = jnp.sum(raw_weights, axis=1, keepdims=True)
    weights = raw_weights.astype(jnp.bfloat16)
    return (
        jnp.einsum("sk,kd->sd", weights, values_all, preferred_element_type=jnp.float32)
        / row_total
    )


def projection_split(n):
    regions, chunks = [], []
    for j in range(n):
        x, z = divmod(j, 16)
        regions.append(x % 2)
        chunks.append((x // 2) * 16 + z)
    return regions, chunks


def owner_of(region_of, chunk_of, region, chunk):
    return [j for j in range(len(region_of)) if region_of[j] == region and chunk_of[j] == chunk][0]


def plane_heads(n):
    assert n == 64
    return -(-HEADS // 4)


def swap_digits(i):
    return (i >> 2) | ((i & 3) << 2)


def head_of(j):
    x, z = j >> 4, j & 15
    head = x * plane_heads(64) + z
    return jnp.where((z < plane_heads(64)) & (head < HEADS), head, HEADS)


def head_placement(n):
    used = plane_heads(n)
    table = []
    for j in range(n):
        x, z = divmod(j, 16)
        head = x * used + z
        table.append(head if z < used and head < HEADS else HEADS)
    return table


def shards(
    query,
    keys,
    values,
    hidden,
    latent,
    deal,
    lengths,
    w_out,
    attn_gate,
    modulation,
    w_final,
    guide,
    step_size,
):
    nseq = lax.axis_size("seq")
    group_id = lax.axis_index("grp")
    branch = lax.axis_index("cfg")
    partner = jnp.bitwise_xor(group_id, 1)
    own_lengths = lax.dynamic_index_in_dim(lengths, group_id, 0, keepdims=False)
    pair_lengths = lax.dynamic_index_in_dim(lengths, partner, 0, keepdims=False)
    item_ids = lax.dynamic_index_in_dim(deal, group_id, 0, keepdims=False)
    local_query = query[0, 0]
    resident_key_rows = keys[0, 0]
    local_values = values[0, 0]
    shard_rows = resident_key_rows.shape[1]
    slot_total = nseq * shard_rows
    far_keys, far_values = from_partner(
        jnp.stack([resident_key_rows[1], local_values[1]]), "grp", 0
    )

    head_table = head_placement(nseq)

    used = plane_heads(nseq)
    planes = nseq // 16

    def to_heads(x):
        n = x.shape[0]
        x = x.reshape(n, shard_rows, HEADS, HD).transpose(2, 0, 1, 3)
        x = jnp.pad(x, ((0, planes * used - HEADS), (0, 0), (0, 0), (0, 0)))
        x = x.reshape(planes, used, n, shard_rows, HD)
        x = jnp.pad(x, ((0, 0), (0, 16 - used), (0, 0), (0, 0), (0, 0)))
        return x.reshape(nseq, n, shard_rows, HD)

    region_of, chunk_of = projection_split(nseq)
    chunks = max(chunk_of) + 1
    block_rows = w_out.shape[0]
    col_width = D // chunks
    w_parts = w_out.reshape(block_rows, chunks, col_width).transpose(1, 0, 2)
    w_parts = w_parts.reshape(planes // 2, 1, 16, block_rows, col_width)
    w_parts = jnp.broadcast_to(w_parts, (planes // 2, 2, 16, block_rows, col_width))
    w_parts = w_parts.reshape(nseq, block_rows, col_width)
    packed = to_heads(
        jnp.concatenate(
            [local_query, resident_key_rows, far_keys[None], local_values, far_values[None]], 0
        )
    )
    head_width = packed.shape[1] * shard_rows * HD
    joint = jnp.concatenate(
        [packed.reshape(nseq, head_width), w_parts.reshape(nseq, block_rows * col_width)], 1
    )
    joint = lax.all_to_all(joint, "seq", 0, 0, tiled=True)
    head_rows = joint[:, :head_width].reshape(nseq, 8, shard_rows, HD)
    head_rows = head_rows.transpose(1, 0, 2, 3).reshape(8, slot_total, HD)
    head_q, head_k, head_v = head_rows[0:2], head_rows[2:5], head_rows[5:8]
    slot_ids = jnp.arange(slot_total)
    live_home = slot_ids < own_lengths[0]
    live_own = slot_ids < own_lengths[1]
    live_pair = slot_ids < pair_lengths[1]
    home_out = head_attend(head_q[0], head_k[0], head_v[0], live_home)
    shared_out = head_attend(
        head_q[1],
        jnp.concatenate([head_k[1], head_k[2]], 0),
        jnp.concatenate([head_v[1], head_v[2]], 0),
        jnp.concatenate([live_own, live_pair], 0),
    )
    head_attn = jnp.stack([home_out, shared_out]).astype(jnp.bfloat16)

    w_half = joint[:, head_width:].reshape(nseq * block_rows, col_width)
    w_other = from_partner(w_half, "cfg", 0)
    w_cols = jnp.where(
        branch == 0,
        jnp.concatenate([w_half, w_other], 0),
        jnp.concatenate([w_other, w_half], 0),
    )

    me = lax.axis_index("seq")
    gathered = head_attn[None]
    masks = [0]
    for low_bit in (2, 0):
        parts = [gathered]
        grown = list(masks)
        for digit in (1, 2, 3):
            shift = digit << low_bit
            parts.append(lax.ppermute(gathered, "seq", [(i, i ^ shift) for i in range(nseq)]))
            grown += [m ^ shift for m in masks]
        gathered = jnp.concatenate(parts, 0)
        masks = grown
    plane = len(masks)
    assert masks == [swap_digits(i) for i in range(len(masks))]
    my_z = me % plane
    my_x = me // plane
    by_z = jnp.take(gathered, swap_digits(jnp.bitwise_xor(my_z, jnp.arange(plane))), axis=0)
    my_region = my_x % 2
    parts = [lax.dynamic_index_in_dim(by_z, my_region, 1, keepdims=False)]
    sources = [my_x * plane + jnp.arange(plane)]
    for digit in (1, 2, 3):
        shift = digit * plane
        outgoing = lax.dynamic_index_in_dim(by_z[:used], (my_x ^ digit) % 2, 1, keepdims=False)
        parts.append(lax.ppermute(outgoing, "seq", [(i, i ^ shift) for i in range(nseq)]))
        sources.append(jnp.bitwise_xor(my_x, digit) * plane + jnp.arange(used))
    gathered = jnp.concatenate(parts, 0)
    source_head = head_of(jnp.concatenate(sources))
    w_heads = jnp.pad(w_cols.reshape(HEADS, HD, col_width), ((0, 1), (0, 0), (0, 0)))
    w_ordered = jnp.take(w_heads, source_head, axis=0)
    projected_cols = jnp.einsum(
        "isd,idc->sc", gathered, w_ordered, preferred_element_type=jnp.float32
    )
    projected_parts = projected_cols.reshape(nseq, shard_rows, col_width)
    received = lax.all_to_all(projected_parts, "seq", 0, 0, tiled=True)
    projected = received.reshape(2, 2, 16, shard_rows, col_width).transpose(1, 3, 0, 2, 4)
    projected = projected.reshape(2, shard_rows, D)

    item_count = guide.shape[0]
    indicator_mask = (jnp.arange(item_count)[None, :] == item_ids[:, None]).astype(jnp.float32)
    gate_now = jnp.einsum(
        "ri,id->rd", indicator_mask, attn_gate[0], precision=lax.Precision.HIGHEST
    )
    stream = hidden[0, 0].astype(jnp.float32) + gate_now[:, None, :] * projected
    row_mean = jnp.mean(stream, axis=2, keepdims=True)
    centred = stream - row_mean
    row_var = jnp.mean(centred * centred, axis=2, keepdims=True)
    normed = centred * lax.rsqrt(row_var + NORM_EPS)
    selected_entries = jnp.einsum(
        "ub,bkg->ukg", indicator_mask, modulation[0], precision=lax.Precision.HIGHEST
    )
    shaped = (
        normed * (1.0 + selected_entries[:, 1][:, None, :]) + selected_entries[:, 0][:, None, :]
    ).astype(jnp.bfloat16)
    velocity = jnp.einsum("rsd,dc->rsc", shaped, w_final, preferred_element_type=jnp.float32)
    row_slots = lax.axis_index("seq") * shard_rows + jnp.arange(shard_rows)
    live_rows = jnp.stack([row_slots < own_lengths[0], row_slots < own_lengths[1]])
    velocity = jnp.where(live_rows[:, :, None], velocity, jnp.float32(0.0))
    weight_now = jnp.sum(indicator_mask * guide[None, :], axis=1)[:, None, None]
    step_now = jnp.sum(indicator_mask * step_size[None, :], axis=1)[:, None, None]
    latent_part = latent[0]
    part_width = latent_part.shape[2]
    outgoing_velocity = lax.dynamic_slice_in_dim(velocity, (1 - branch) * part_width, part_width, 2)
    own_velocity = lax.dynamic_slice_in_dim(velocity, branch * part_width, part_width, 2)
    other_velocity = from_partner(outgoing_velocity, "cfg", 0)
    is_conditional = branch == 0
    cond_velocity = jnp.where(is_conditional, own_velocity, other_velocity)
    uncond_velocity = jnp.where(is_conditional, other_velocity, own_velocity)
    guided = uncond_velocity + weight_now * (cond_velocity - uncond_velocity)
    updated = latent_part - step_now * guided
    return updated[None]


def solution(mesh):
    placed = (
        P("cfg", "grp", None, "seq", None),
        P("cfg", "grp", None, "seq", None),
        P("cfg", "grp", None, "seq", None),
        P("cfg", "grp", None, "seq", None),
        P("grp", None, "seq", "cfg"),
        P(),
        P(),
        P(("cfg", "seq"), None),
        P("cfg", None, None),
        P("cfg", None, None, None),
        P(),
        P(),
        P(),
    )
    return jax.shard_map(
        shards, mesh=mesh, in_specs=placed, out_specs=P("grp", None, "seq", "cfg"), check_vma=False
    )
```

```python
import jax
import jax.numpy as jnp
from jax import lax
from jax.sharding import PartitionSpec as P

D = 2432
HEADS = 38
HD = 64


NORM_EPS = 1e-06


def from_partner(x, axis, apart):
    return lax.ppermute(x, axis, [(i, i ^ 1 << apart) for i in range(lax.axis_size(axis))])


def head_attend(queries, keys_all, values_all, live_keys):
    scores = jnp.einsum(
        "sd,kd->sk", queries, keys_all, preferred_element_type=jnp.float32
    ) * HD ** (-0.5)
    scores = jnp.where(live_keys[None, :], scores, -jnp.inf)
    peak_score = jnp.max(scores, axis=1, keepdims=True)
    raw_weights = jnp.exp(scores - peak_score)
    row_total = jnp.sum(raw_weights, axis=1, keepdims=True)
    weights = raw_weights.astype(jnp.bfloat16)
    return (
        jnp.einsum("sk,kd->sd", weights, values_all, preferred_element_type=jnp.float32)
        / row_total
    )


def projection_split(n):
    regions, chunks = [], []
    for j in range(n):
        x, z = divmod(j, 16)
        regions.append(x % 2)
        chunks.append((x // 2) * 16 + z)
    return regions, chunks


def owner_of(region_of, chunk_of, region, chunk):
    return [j for j in range(len(region_of)) if region_of[j] == region and chunk_of[j] == chunk][0]


def plane_heads(n):
    assert n == 64
    return -(-HEADS // 4)


def swap_digits(i):
    return (i >> 2) | ((i & 3) << 2)


def head_of(j):
    x, z = j >> 4, j & 15
    head = x * plane_heads(64) + z
    return jnp.where((z < plane_heads(64)) & (head < HEADS), head, HEADS)


def head_placement(n):
    used = plane_heads(n)
    table = []
    for j in range(n):
        x, z = divmod(j, 16)
        head = x * used + z
        table.append(head if z < used and head < HEADS else HEADS)
    return table


def shards(
    query,
    keys,
    values,
    hidden,
    latent,
    deal,
    lengths,
    w_out,
    attn_gate,
    modulation,
    w_final,
    guide,
    step_size,
):
    nseq = lax.axis_size("seq")
    group_id = lax.axis_index("grp")
    branch = lax.axis_index("cfg")
    partner = jnp.bitwise_xor(group_id, 1)
    own_lengths = lax.dynamic_index_in_dim(lengths, group_id, 0, keepdims=False)
    pair_lengths = lax.dynamic_index_in_dim(lengths, partner, 0, keepdims=False)
    item_ids = lax.dynamic_index_in_dim(deal, group_id, 0, keepdims=False)
    local_query = query[0, 0]
    resident_key_rows = keys[0, 0]
    local_values = values[0, 0]
    shard_rows = resident_key_rows.shape[1]
    slot_total = nseq * shard_rows
    far_keys, far_values = from_partner(
        jnp.stack([resident_key_rows[1], local_values[1]]), "grp", 0
    )

    head_table = head_placement(nseq)

    used = plane_heads(nseq)
    planes = nseq // 16

    def to_heads(x):
        n = x.shape[0]
        x = x.reshape(n, shard_rows, HEADS, HD).transpose(2, 0, 1, 3)
        x = jnp.pad(x, ((0, planes * used - HEADS), (0, 0), (0, 0), (0, 0)))
        x = x.reshape(planes, used, n, shard_rows, HD)
        x = jnp.pad(x, ((0, 0), (0, 16 - used), (0, 0), (0, 0), (0, 0)))
        return x.reshape(nseq, n, shard_rows, HD)

    region_of, chunk_of = projection_split(nseq)
    chunks = max(chunk_of) + 1
    block_rows = w_out.shape[0]
    col_width = D // chunks
    half_width = col_width // 2
    w_parts = w_out.reshape(block_rows, planes // 2, 16, 2, half_width).transpose(1, 3, 2, 0, 4)
    w_parts = w_parts.reshape(nseq, block_rows, half_width)
    packed = to_heads(
        jnp.concatenate(
            [local_query, resident_key_rows, far_keys[None], local_values, far_values[None]], 0
        )
    )
    head_width = packed.shape[1] * shard_rows * HD
    joint = jnp.concatenate(
        [packed.reshape(nseq, head_width), w_parts.reshape(nseq, block_rows * half_width)], 1
    )
    joint = lax.all_to_all(joint, "seq", 0, 0, tiled=True)
    head_rows = joint[:, :head_width].reshape(nseq, 8, shard_rows, HD)
    head_rows = head_rows.transpose(1, 0, 2, 3).reshape(8, slot_total, HD)
    head_q, head_k, head_v = head_rows[0:2], head_rows[2:5], head_rows[5:8]
    slot_ids = jnp.arange(slot_total)
    live_home = slot_ids < own_lengths[0]
    live_own = slot_ids < own_lengths[1]
    live_pair = slot_ids < pair_lengths[1]
    home_out = head_attend(head_q[0], head_k[0], head_v[0], live_home)
    shared_out = head_attend(
        head_q[1],
        jnp.concatenate([head_k[1], head_k[2]], 0),
        jnp.concatenate([head_v[1], head_v[2]], 0),
        jnp.concatenate([live_own, live_pair], 0),
    )
    head_attn = jnp.stack([home_out, shared_out]).astype(jnp.bfloat16)

    w_half = joint[:, head_width:].reshape(nseq * block_rows, half_width)
    w_other = from_partner(w_half, "cfg", 0)
    w_quarter = jnp.where(
        branch == 0,
        jnp.concatenate([w_half, w_other], 0),
        jnp.concatenate([w_other, w_half], 0),
    )

    me = lax.axis_index("seq")
    gathered = head_attn[None]
    masks = [0]
    for low_bit in (2, 0):
        parts = [gathered]
        grown = list(masks)
        for digit in (1, 2, 3):
            shift = digit << low_bit
            parts.append(lax.ppermute(gathered, "seq", [(i, i ^ shift) for i in range(nseq)]))
            grown += [m ^ shift for m in masks]
        gathered = jnp.concatenate(parts, 0)
        masks = grown
    plane = len(masks)
    assert masks == [swap_digits(i) for i in range(len(masks))]
    my_z = me % plane
    my_x = me // plane
    by_z = jnp.take(gathered, swap_digits(jnp.bitwise_xor(my_z, jnp.arange(plane))), axis=0)
    my_region = my_x % 2
    parts = [lax.dynamic_index_in_dim(by_z, my_region, 1, keepdims=False)]
    sources = [my_x * plane + jnp.arange(plane)]
    for digit in (1, 2, 3):
        shift = digit * plane
        outgoing = lax.dynamic_index_in_dim(by_z[:used], (my_x ^ digit) % 2, 1, keepdims=False)
        pairs = [(i, i ^ shift) for i in range(nseq)]
        if digit == 1:
            block_size = outgoing.size
            both = lax.ppermute(
                jnp.concatenate([outgoing.reshape(-1), w_quarter.reshape(-1)]), "seq", pairs
            )
            parts.append(both[:block_size].reshape(outgoing.shape))
            w_partner = both[block_size:].reshape(w_quarter.shape)
        else:
            parts.append(lax.ppermute(outgoing, "seq", pairs))
        sources.append(jnp.bitwise_xor(my_x, digit) * plane + jnp.arange(used))
    gathered = jnp.concatenate(parts, 0)
    w_cols = jnp.where(
        my_region == 0,
        jnp.concatenate([w_quarter, w_partner], 1),
        jnp.concatenate([w_partner, w_quarter], 1),
    )
    source_head = head_of(jnp.concatenate(sources))
    w_heads = jnp.pad(w_cols.reshape(HEADS, HD, col_width), ((0, 1), (0, 0), (0, 0)))
    w_ordered = jnp.take(w_heads, source_head, axis=0)
    projected_cols = jnp.einsum(
        "isd,idc->sc", gathered, w_ordered, preferred_element_type=jnp.float32
    )
    projected_parts = projected_cols.reshape(nseq, shard_rows, col_width)
    received = lax.all_to_all(projected_parts, "seq", 0, 0, tiled=True)
    projected = received.reshape(2, 2, 16, shard_rows, col_width).transpose(1, 3, 0, 2, 4)
    projected = projected.reshape(2, shard_rows, D)

    item_count = guide.shape[0]
    indicator_mask = (jnp.arange(item_count)[None, :] == item_ids[:, None]).astype(jnp.float32)
    gate_now = jnp.einsum(
        "ri,id->rd", indicator_mask, attn_gate[0], precision=lax.Precision.HIGHEST
    )
    stream = hidden[0, 0].astype(jnp.float32) + gate_now[:, None, :] * projected
    row_mean = jnp.mean(stream, axis=2, keepdims=True)
    centred = stream - row_mean
    row_var = jnp.mean(centred * centred, axis=2, keepdims=True)
    normed = centred * lax.rsqrt(row_var + NORM_EPS)
    selected_entries = jnp.einsum(
        "ub,bkg->ukg", indicator_mask, modulation[0], precision=lax.Precision.HIGHEST
    )
    shaped = (
        normed * (1.0 + selected_entries[:, 1][:, None, :]) + selected_entries[:, 0][:, None, :]
    ).astype(jnp.bfloat16)
    velocity = jnp.einsum("rsd,dc->rsc", shaped, w_final, preferred_element_type=jnp.float32)
    row_slots = lax.axis_index("seq") * shard_rows + jnp.arange(shard_rows)
    live_rows = jnp.stack([row_slots < own_lengths[0], row_slots < own_lengths[1]])
    velocity = jnp.where(live_rows[:, :, None], velocity, jnp.float32(0.0))
    weight_now = jnp.sum(indicator_mask * guide[None, :], axis=1)[:, None, None]
    step_now = jnp.sum(indicator_mask * step_size[None, :], axis=1)[:, None, None]
    latent_part = latent[0]
    part_width = latent_part.shape[2]
    outgoing_velocity = lax.dynamic_slice_in_dim(velocity, (1 - branch) * part_width, part_width, 2)
    own_velocity = lax.dynamic_slice_in_dim(velocity, branch * part_width, part_width, 2)
    other_velocity = from_partner(outgoing_velocity, "cfg", 0)
    is_conditional = branch == 0
    cond_velocity = jnp.where(is_conditional, own_velocity, other_velocity)
    uncond_velocity = jnp.where(is_conditional, other_velocity, own_velocity)
    guided = uncond_velocity + weight_now * (cond_velocity - uncond_velocity)
    updated = latent_part - step_now * guided
    return updated[None]


def solution(mesh):
    placed = (
        P("cfg", "grp", None, "seq", None),
        P("cfg", "grp", None, "seq", None),
        P("cfg", "grp", None, "seq", None),
        P("cfg", "grp", None, "seq", None),
        P("grp", None, "seq", "cfg"),
        P(),
        P(),
        P(("cfg", "seq"), None),
        P("cfg", None, None),
        P("cfg", None, None, None),
        P(),
        P(),
        P(),
    )
    return jax.shard_map(
        shards, mesh=mesh, in_specs=placed, out_specs=P("grp", None, "seq", "cfg"), check_vma=False
    )
```

```python
import jax
import jax.numpy as jnp
from jax import lax
from jax.sharding import PartitionSpec as P

D = 2432
HEADS = 38
HD = 64


NORM_EPS = 1e-06


def from_partner(x, axis, apart):
    return lax.ppermute(x, axis, [(i, i ^ 1 << apart) for i in range(lax.axis_size(axis))])


def head_attend(queries, keys_all, values_all, live_keys):
    scores = jnp.einsum(
        "sd,kd->sk", queries, keys_all, preferred_element_type=jnp.float32
    ) * HD ** (-0.5)
    scores = jnp.where(live_keys[None, :], scores, -jnp.inf)
    peak_score = jnp.max(scores, axis=1, keepdims=True)
    raw_weights = jnp.exp(scores - peak_score)
    row_total = jnp.sum(raw_weights, axis=1, keepdims=True)
    weights = raw_weights.astype(jnp.bfloat16)
    return (
        jnp.einsum("sk,kd->sd", weights, values_all, preferred_element_type=jnp.float32)
        / row_total
    )


def projection_split(n):
    regions, chunks = [], []
    for j in range(n):
        x, z = divmod(j, 16)
        regions.append(x % 2)
        chunks.append((x // 2) * 16 + z)
    return regions, chunks


def owner_of(region_of, chunk_of, region, chunk):
    return [j for j in range(len(region_of)) if region_of[j] == region and chunk_of[j] == chunk][0]


def plane_heads(n):
    assert n == 64
    return -(-HEADS // 4)


def swap_digits(i):
    return (i >> 2) | ((i & 3) << 2)


def head_of(j):
    x, z = j >> 4, j & 15
    head = x * plane_heads(64) + z
    return jnp.where((z < plane_heads(64)) & (head < HEADS), head, HEADS)


def head_placement(n):
    used = plane_heads(n)
    table = []
    for j in range(n):
        x, z = divmod(j, 16)
        head = x * used + z
        table.append(head if z < used and head < HEADS else HEADS)
    return table


def shards(
    query,
    keys,
    values,
    hidden,
    latent,
    deal,
    lengths,
    w_out,
    attn_gate,
    modulation,
    w_final,
    guide,
    step_size,
):
    nseq = lax.axis_size("seq")
    group_id = lax.axis_index("grp")
    branch = lax.axis_index("cfg")
    partner = jnp.bitwise_xor(group_id, 1)
    own_lengths = lax.dynamic_index_in_dim(lengths, group_id, 0, keepdims=False)
    pair_lengths = lax.dynamic_index_in_dim(lengths, partner, 0, keepdims=False)
    item_ids = lax.dynamic_index_in_dim(deal, group_id, 0, keepdims=False)
    local_query = query[0, 0]
    resident_key_rows = keys[0, 0]
    local_values = values[0, 0]
    shard_rows = resident_key_rows.shape[1]
    slot_total = nseq * shard_rows
    far_keys, far_values = from_partner(
        jnp.stack([resident_key_rows[1], local_values[1]]), "grp", 0
    )

    head_table = head_placement(nseq)

    used = plane_heads(nseq)
    planes = nseq // 16

    def to_heads(x):
        n = x.shape[0]
        x = x.reshape(n, shard_rows, HEADS, HD).transpose(2, 0, 1, 3)
        x = jnp.pad(x, ((0, planes * used - HEADS), (0, 0), (0, 0), (0, 0)))
        x = x.reshape(planes, used, n, shard_rows, HD)
        x = jnp.pad(x, ((0, 0), (0, 16 - used), (0, 0), (0, 0), (0, 0)))
        return x.reshape(nseq, n, shard_rows, HD)

    region_of, chunk_of = projection_split(nseq)
    chunks = max(chunk_of) + 1
    block_rows = w_out.shape[0]
    col_width = D // chunks
    half_width = col_width // 2
    w_parts = w_out.reshape(block_rows, planes // 2, 16, 2, half_width).transpose(1, 3, 2, 0, 4)
    w_parts = w_parts.reshape(nseq, block_rows, half_width)
    packed = to_heads(
        jnp.concatenate(
            [local_query, resident_key_rows, far_keys[None], local_values, far_values[None]], 0
        )
    )
    head_width = packed.shape[1] * shard_rows * HD
    joint = jnp.concatenate(
        [packed.reshape(nseq, head_width), w_parts.reshape(nseq, block_rows * half_width)], 1
    )
    joint = lax.all_to_all(joint, "seq", 0, 0, tiled=True)
    head_rows = joint[:, :head_width].reshape(nseq, 8, shard_rows, HD)
    head_rows = head_rows.transpose(1, 0, 2, 3).reshape(8, slot_total, HD)
    head_q, head_k, head_v = head_rows[0:2], head_rows[2:5], head_rows[5:8]
    key_ids = jnp.arange(2 * slot_total)
    live_home = key_ids[:slot_total] < own_lengths[0]
    live_shared = key_ids < jnp.where(
        key_ids < slot_total, own_lengths[1], slot_total + pair_lengths[1]
    )
    home_out = head_attend(head_q[0], head_k[0], head_v[0], live_home)
    shared_out = head_attend(
        head_q[1],
        head_k[1:3].reshape(2 * slot_total, HD),
        head_v[1:3].reshape(2 * slot_total, HD),
        live_shared,
    )
    head_attn = jnp.stack([home_out, shared_out]).astype(jnp.bfloat16)

    w_half = joint[:, head_width:].reshape(nseq * block_rows, half_width)
    w_other = from_partner(w_half, "cfg", 0)
    w_quarter = jnp.where(
        branch == 0,
        jnp.concatenate([w_half, w_other], 0),
        jnp.concatenate([w_other, w_half], 0),
    )

    me = lax.axis_index("seq")
    gathered = head_attn[None]
    masks = [0]
    for low_bit in (2, 0):
        parts = [gathered]
        grown = list(masks)
        for digit in (1, 2, 3):
            shift = digit << low_bit
            parts.append(lax.ppermute(gathered, "seq", [(i, i ^ shift) for i in range(nseq)]))
            grown += [m ^ shift for m in masks]
        gathered = jnp.concatenate(parts, 0)
        masks = grown
    plane = len(masks)
    assert masks == [swap_digits(i) for i in range(len(masks))]
    my_z = me % plane
    my_x = me // plane
    by_z = jnp.take(gathered, swap_digits(jnp.bitwise_xor(my_z, jnp.arange(plane))), axis=0)
    my_region = my_x % 2
    parts = [lax.dynamic_index_in_dim(by_z, my_region, 1, keepdims=False)]
    sources = [my_x * plane + jnp.arange(plane)]
    for digit in (1, 2, 3):
        shift = digit * plane
        outgoing = lax.dynamic_index_in_dim(by_z[:used], (my_x ^ digit) % 2, 1, keepdims=False)
        pairs = [(i, i ^ shift) for i in range(nseq)]
        if digit == 1:
            block_size = outgoing.size
            both = lax.ppermute(
                jnp.concatenate([outgoing.reshape(-1), w_quarter.reshape(-1)]), "seq", pairs
            )
            parts.append(both[:block_size].reshape(outgoing.shape))
            w_partner = both[block_size:].reshape(w_quarter.shape)
        else:
            parts.append(lax.ppermute(outgoing, "seq", pairs))
        sources.append(jnp.bitwise_xor(my_x, digit) * plane + jnp.arange(used))
    gathered = jnp.concatenate(parts, 0)
    w_cols = jnp.where(
        my_region == 0,
        jnp.concatenate([w_quarter, w_partner], 1),
        jnp.concatenate([w_partner, w_quarter], 1),
    )
    source_head = head_of(jnp.concatenate(sources))
    w_heads = jnp.pad(w_cols.reshape(HEADS, HD, col_width), ((0, 1), (0, 0), (0, 0)))
    w_ordered = jnp.take(w_heads, source_head, axis=0)
    projected_cols = jnp.einsum(
        "isd,idc->sc", gathered, w_ordered, preferred_element_type=jnp.float32
    )
    projected_parts = projected_cols.reshape(nseq, shard_rows, col_width)
    received = lax.all_to_all(projected_parts, "seq", 0, 0, tiled=True)
    projected = received.reshape(2, 2, 16, shard_rows, col_width).transpose(1, 3, 0, 2, 4)
    projected = projected.reshape(2, shard_rows, D)

    item_count = guide.shape[0]
    indicator_mask = (jnp.arange(item_count)[None, :] == item_ids[:, None]).astype(jnp.float32)
    gate_now = jnp.einsum(
        "ri,id->rd", indicator_mask, attn_gate[0], precision=lax.Precision.HIGHEST
    )
    stream = hidden[0, 0].astype(jnp.float32) + gate_now[:, None, :] * projected
    row_mean = jnp.mean(stream, axis=2, keepdims=True)
    centred = stream - row_mean
    row_var = jnp.mean(centred * centred, axis=2, keepdims=True)
    normed = centred * lax.rsqrt(row_var + NORM_EPS)
    selected_entries = jnp.einsum(
        "ub,bkg->ukg", indicator_mask, modulation[0], precision=lax.Precision.HIGHEST
    )
    shaped = (
        normed * (1.0 + selected_entries[:, 1][:, None, :]) + selected_entries[:, 0][:, None, :]
    ).astype(jnp.bfloat16)
    velocity = jnp.einsum("rsd,dc->rsc", shaped, w_final, preferred_element_type=jnp.float32)
    row_slots = lax.axis_index("seq") * shard_rows + jnp.arange(shard_rows)
    live_rows = jnp.stack([row_slots < own_lengths[0], row_slots < own_lengths[1]])
    velocity = jnp.where(live_rows[:, :, None], velocity, jnp.float32(0.0))
    weight_now = jnp.sum(indicator_mask * guide[None, :], axis=1)[:, None, None]
    step_now = jnp.sum(indicator_mask * step_size[None, :], axis=1)[:, None, None]
    latent_part = latent[0]
    part_width = latent_part.shape[2]
    outgoing_velocity = lax.dynamic_slice_in_dim(velocity, (1 - branch) * part_width, part_width, 2)
    own_velocity = lax.dynamic_slice_in_dim(velocity, branch * part_width, part_width, 2)
    other_velocity = from_partner(outgoing_velocity, "cfg", 0)
    is_conditional = branch == 0
    cond_velocity = jnp.where(is_conditional, own_velocity, other_velocity)
    uncond_velocity = jnp.where(is_conditional, other_velocity, own_velocity)
    guided = uncond_velocity + weight_now * (cond_velocity - uncond_velocity)
    updated = latent_part - step_now * guided
    return updated[None]


def solution(mesh):
    placed = (
        P("cfg", "grp", None, "seq", None),
        P("cfg", "grp", None, "seq", None),
        P("cfg", "grp", None, "seq", None),
        P("cfg", "grp", None, "seq", None),
        P("grp", None, "seq", "cfg"),
        P(),
        P(),
        P(("cfg", "seq"), None),
        P("cfg", None, None),
        P("cfg", None, None, None),
        P(),
        P(),
        P(),
    )
    return jax.shard_map(
        shards, mesh=mesh, in_specs=placed, out_specs=P("grp", None, "seq", "cfg"), check_vma=False
    )
```

```python
import jax
import jax.numpy as jnp
from jax import lax
from jax.sharding import PartitionSpec as P

D = 2432
HEADS = 38
HD = 64


NORM_EPS = 1e-06


def from_partner(x, axis, apart):
    return lax.ppermute(x, axis, [(i, i ^ 1 << apart) for i in range(lax.axis_size(axis))])


def head_attend(queries, keys_all, values_all, live_keys):
    scores = jnp.einsum(
        "sd,kd->sk", queries, keys_all, preferred_element_type=jnp.float32
    ) * HD ** (-0.5)
    scores = jnp.where(live_keys[None, :], scores, -jnp.inf)
    peak_score = jnp.max(scores, axis=1, keepdims=True)
    raw_weights = jnp.exp(scores - peak_score)
    row_total = jnp.sum(raw_weights, axis=1, keepdims=True)
    weights = raw_weights.astype(jnp.bfloat16)
    return (
        jnp.einsum("sk,kd->sd", weights, values_all, preferred_element_type=jnp.float32)
        / row_total
    )


def projection_split(n):
    regions, chunks = [], []
    for j in range(n):
        x, z = divmod(j, 16)
        regions.append(x % 2)
        chunks.append((x // 2) * 16 + z)
    return regions, chunks


def owner_of(region_of, chunk_of, region, chunk):
    return [j for j in range(len(region_of)) if region_of[j] == region and chunk_of[j] == chunk][0]


def plane_heads(n):
    assert n == 64
    return -(-HEADS // 4)


def swap_digits(i):
    return (i >> 2) | ((i & 3) << 2)


def head_of(j):
    x, z = j >> 4, j & 15
    head = x * plane_heads(64) + z
    return jnp.where((z < plane_heads(64)) & (head < HEADS), head, HEADS)


def head_placement(n):
    used = plane_heads(n)
    table = []
    for j in range(n):
        x, z = divmod(j, 16)
        head = x * used + z
        table.append(head if z < used and head < HEADS else HEADS)
    return table


def shards(
    query,
    keys,
    values,
    hidden,
    latent,
    deal,
    lengths,
    w_out,
    attn_gate,
    modulation,
    w_final,
    guide,
    step_size,
):
    nseq = lax.axis_size("seq")
    group_id = lax.axis_index("grp")
    branch = lax.axis_index("cfg")
    partner = jnp.bitwise_xor(group_id, 1)
    own_lengths = lax.dynamic_index_in_dim(lengths, group_id, 0, keepdims=False)
    pair_lengths = lax.dynamic_index_in_dim(lengths, partner, 0, keepdims=False)
    item_ids = lax.dynamic_index_in_dim(deal, group_id, 0, keepdims=False)
    local_query = query[0, 0]
    resident_key_rows = keys[0, 0]
    local_values = values[0, 0]
    shard_rows = resident_key_rows.shape[1]
    slot_total = nseq * shard_rows
    far_keys, far_values = from_partner(
        jnp.stack([resident_key_rows[1], local_values[1]]), "grp", 0
    )

    head_table = head_placement(nseq)

    used = plane_heads(nseq)
    planes = nseq // 16

    def to_heads(x):
        n = x.shape[0]
        x = jnp.pad(x, ((0, 0), (0, 0), (0, (planes * used - HEADS) * HD)))
        x = x.reshape(n, shard_rows, planes, used, HD)
        x = jnp.pad(x, ((0, 0), (0, 0), (0, 0), (0, 16 - used), (0, 0)))
        return x.reshape(n, shard_rows, nseq, HD).transpose(2, 0, 1, 3)

    region_of, chunk_of = projection_split(nseq)
    chunks = max(chunk_of) + 1
    block_rows = w_out.shape[0]
    col_width = D // chunks
    half_width = col_width // 2
    w_parts = w_out.reshape(block_rows, planes // 2, 16, 2, half_width).transpose(1, 3, 2, 0, 4)
    w_parts = w_parts.reshape(nseq, block_rows, half_width)
    packed = to_heads(
        jnp.concatenate(
            [local_query, resident_key_rows, far_keys[None], local_values, far_values[None]], 0
        )
    )
    head_width = packed.shape[1] * shard_rows * HD
    joint = jnp.concatenate(
        [packed.reshape(nseq, head_width), w_parts.reshape(nseq, block_rows * half_width)], 1
    )
    joint = lax.all_to_all(joint, "seq", 0, 0, tiled=True)
    head_rows = joint[:, :head_width].reshape(nseq, 8, shard_rows, HD)
    head_rows = head_rows.transpose(1, 0, 2, 3).reshape(8, slot_total, HD)
    head_q, head_k, head_v = head_rows[0:2], head_rows[2:5], head_rows[5:8]
    key_ids = jnp.arange(2 * slot_total)
    live_home = key_ids[:slot_total] < own_lengths[0]
    live_shared = key_ids < jnp.where(
        key_ids < slot_total, own_lengths[1], slot_total + pair_lengths[1]
    )
    home_out = head_attend(head_q[0], head_k[0], head_v[0], live_home)
    shared_out = head_attend(
        head_q[1],
        head_k[1:3].reshape(2 * slot_total, HD),
        head_v[1:3].reshape(2 * slot_total, HD),
        live_shared,
    )
    head_attn = jnp.stack([home_out, shared_out]).astype(jnp.bfloat16)

    w_half = joint[:, head_width:].reshape(nseq * block_rows, half_width)
    w_other = from_partner(w_half, "cfg", 0)
    w_quarter = jnp.where(
        branch == 0,
        jnp.concatenate([w_half, w_other], 0),
        jnp.concatenate([w_other, w_half], 0),
    )

    me = lax.axis_index("seq")
    gathered = head_attn[None]
    masks = [0]
    for low_bit in (2, 0):
        parts = [gathered]
        grown = list(masks)
        for digit in (1, 2, 3):
            shift = digit << low_bit
            parts.append(lax.ppermute(gathered, "seq", [(i, i ^ shift) for i in range(nseq)]))
            grown += [m ^ shift for m in masks]
        gathered = jnp.concatenate(parts, 0)
        masks = grown
    plane = len(masks)
    assert masks == [swap_digits(i) for i in range(len(masks))]
    my_z = me % plane
    my_x = me // plane
    by_z = jnp.take(gathered, swap_digits(jnp.bitwise_xor(my_z, jnp.arange(plane))), axis=0)
    my_region = my_x % 2
    parts = [lax.dynamic_index_in_dim(by_z, my_region, 1, keepdims=False)]
    sources = [my_x * plane + jnp.arange(plane)]
    for digit in (1, 2, 3):
        shift = digit * plane
        outgoing = lax.dynamic_index_in_dim(by_z[:used], (my_x ^ digit) % 2, 1, keepdims=False)
        pairs = [(i, i ^ shift) for i in range(nseq)]
        if digit == 1:
            block_size = outgoing.size
            both = lax.ppermute(
                jnp.concatenate([outgoing.reshape(-1), w_quarter.reshape(-1)]), "seq", pairs
            )
            parts.append(both[:block_size].reshape(outgoing.shape))
            w_partner = both[block_size:].reshape(w_quarter.shape)
        else:
            parts.append(lax.ppermute(outgoing, "seq", pairs))
        sources.append(jnp.bitwise_xor(my_x, digit) * plane + jnp.arange(used))
    gathered = jnp.concatenate(parts, 0)
    w_cols = jnp.where(
        my_region == 0,
        jnp.concatenate([w_quarter, w_partner], 1),
        jnp.concatenate([w_partner, w_quarter], 1),
    )
    source_head = head_of(jnp.concatenate(sources))
    w_heads = jnp.pad(w_cols.reshape(HEADS, HD, col_width), ((0, 1), (0, 0), (0, 0)))
    w_ordered = jnp.take(w_heads, source_head, axis=0)
    projected_cols = jnp.einsum(
        "isd,idc->sc", gathered, w_ordered, preferred_element_type=jnp.float32
    )
    projected_parts = projected_cols.reshape(nseq, shard_rows, col_width)
    received = lax.all_to_all(projected_parts, "seq", 0, 0, tiled=True)
    projected = received.reshape(2, 2, 16, shard_rows, col_width).transpose(1, 3, 0, 2, 4)
    projected = projected.reshape(2, shard_rows, D)

    item_count = guide.shape[0]
    indicator_mask = (jnp.arange(item_count)[None, :] == item_ids[:, None]).astype(jnp.float32)
    gate_now = jnp.einsum(
        "ri,id->rd", indicator_mask, attn_gate[0], precision=lax.Precision.HIGHEST
    )
    stream = hidden[0, 0].astype(jnp.float32) + gate_now[:, None, :] * projected
    row_mean = jnp.mean(stream, axis=2, keepdims=True)
    centred = stream - row_mean
    row_var = jnp.mean(centred * centred, axis=2, keepdims=True)
    normed = centred * lax.rsqrt(row_var + NORM_EPS)
    selected_entries = jnp.einsum(
        "ub,bkg->ukg", indicator_mask, modulation[0], precision=lax.Precision.HIGHEST
    )
    shaped = (
        normed * (1.0 + selected_entries[:, 1][:, None, :]) + selected_entries[:, 0][:, None, :]
    ).astype(jnp.bfloat16)
    velocity = jnp.einsum("rsd,dc->rsc", shaped, w_final, preferred_element_type=jnp.float32)
    row_slots = lax.axis_index("seq") * shard_rows + jnp.arange(shard_rows)
    live_rows = jnp.stack([row_slots < own_lengths[0], row_slots < own_lengths[1]])
    velocity = jnp.where(live_rows[:, :, None], velocity, jnp.float32(0.0))
    weight_now = jnp.sum(indicator_mask * guide[None, :], axis=1)[:, None, None]
    step_now = jnp.sum(indicator_mask * step_size[None, :], axis=1)[:, None, None]
    latent_part = latent[0]
    part_width = latent_part.shape[2]
    outgoing_velocity = lax.dynamic_slice_in_dim(velocity, (1 - branch) * part_width, part_width, 2)
    own_velocity = lax.dynamic_slice_in_dim(velocity, branch * part_width, part_width, 2)
    other_velocity = from_partner(outgoing_velocity, "cfg", 0)
    is_conditional = branch == 0
    cond_velocity = jnp.where(is_conditional, own_velocity, other_velocity)
    uncond_velocity = jnp.where(is_conditional, other_velocity, own_velocity)
    guided = uncond_velocity + weight_now * (cond_velocity - uncond_velocity)
    updated = latent_part - step_now * guided
    return updated[None]


def solution(mesh):
    placed = (
        P("cfg", "grp", None, "seq", None),
        P("cfg", "grp", None, "seq", None),
        P("cfg", "grp", None, "seq", None),
        P("cfg", "grp", None, "seq", None),
        P("grp", None, "seq", "cfg"),
        P(),
        P(),
        P(("cfg", "seq"), None),
        P("cfg", None, None),
        P("cfg", None, None, None),
        P(),
        P(),
        P(),
    )
    return jax.shard_map(
        shards, mesh=mesh, in_specs=placed, out_specs=P("grp", None, "seq", "cfg"), check_vma=False
    )
```

```python
import jax
import jax.numpy as jnp
from jax import lax
from jax.sharding import PartitionSpec as P

D = 2432
HEADS = 38
HD = 64


NORM_EPS = 1e-06


def from_partner(x, axis, apart):
    return lax.ppermute(x, axis, [(i, i ^ 1 << apart) for i in range(lax.axis_size(axis))])


def head_attend(queries, keys_all, values_all, live_keys):
    scores = jnp.einsum(
        "sd,kd->sk", queries, keys_all, preferred_element_type=jnp.float32
    ) * HD ** (-0.5)
    scores = jnp.where(live_keys[None, :], scores, -jnp.inf)
    peak_score = jnp.max(scores, axis=1, keepdims=True)
    raw_weights = jnp.exp(scores - peak_score)
    row_total = jnp.sum(raw_weights, axis=1, keepdims=True)
    weights = raw_weights.astype(jnp.bfloat16)
    return (
        jnp.einsum("sk,kd->sd", weights, values_all, preferred_element_type=jnp.float32)
        / row_total
    )


def projection_split(n):
    regions, chunks = [], []
    for j in range(n):
        x, z = divmod(j, 16)
        regions.append(x % 2)
        chunks.append((x // 2) * 16 + z)
    return regions, chunks


def owner_of(region_of, chunk_of, region, chunk):
    return [j for j in range(len(region_of)) if region_of[j] == region and chunk_of[j] == chunk][0]


def plane_heads(n):
    assert n == 64
    return -(-HEADS // 4)


def swap_digits(i):
    return (i >> 2) | ((i & 3) << 2)


def head_of(j):
    x, z = j >> 4, j & 15
    head = x * plane_heads(64) + z
    return jnp.where((z < plane_heads(64)) & (head < HEADS), head, HEADS)


def head_placement(n):
    used = plane_heads(n)
    table = []
    for j in range(n):
        x, z = divmod(j, 16)
        head = x * used + z
        table.append(head if z < used and head < HEADS else HEADS)
    return table


def shards(
    query,
    keys,
    values,
    hidden,
    latent,
    deal,
    lengths,
    w_out,
    attn_gate,
    modulation,
    w_final,
    guide,
    step_size,
):
    nseq = lax.axis_size("seq")
    group_id = lax.axis_index("grp")
    branch = lax.axis_index("cfg")
    partner = jnp.bitwise_xor(group_id, 1)
    own_lengths = lax.dynamic_index_in_dim(lengths, group_id, 0, keepdims=False)
    pair_lengths = lax.dynamic_index_in_dim(lengths, partner, 0, keepdims=False)
    item_ids = lax.dynamic_index_in_dim(deal, group_id, 0, keepdims=False)
    local_query = query[0, 0]
    resident_key_rows = keys[0, 0]
    local_values = values[0, 0]
    shard_rows = resident_key_rows.shape[1]
    slot_total = nseq * shard_rows
    far_keys, far_values = from_partner(
        jnp.stack([resident_key_rows[1], local_values[1]]), "grp", 0
    )

    head_table = head_placement(nseq)

    used = plane_heads(nseq)
    planes = nseq // 16

    def to_heads(x):
        n = x.shape[0]
        x = jnp.pad(x, ((0, 0), (0, 0), (0, (planes * used - HEADS) * HD)))
        x = x.reshape(n, shard_rows, planes, used, HD)
        x = jnp.pad(x, ((0, 0), (0, 0), (0, 0), (0, 16 - used), (0, 0)))
        return x.reshape(n, shard_rows, nseq, HD).transpose(2, 0, 1, 3)

    region_of, chunk_of = projection_split(nseq)
    chunks = max(chunk_of) + 1
    block_rows = w_out.shape[0]
    col_width = D // chunks
    half_width = col_width // 2
    w_parts = w_out.reshape(block_rows, planes // 2, 16, 2, half_width).transpose(1, 3, 2, 0, 4)
    w_parts = w_parts.reshape(nseq, block_rows, half_width)
    packed = to_heads(
        jnp.concatenate(
            [local_query, resident_key_rows, far_keys[None], local_values, far_values[None]], 0
        )
    )
    head_width = packed.shape[1] * shard_rows * HD
    joint = jnp.concatenate(
        [packed.reshape(nseq, head_width), w_parts.reshape(nseq, block_rows * half_width)], 1
    )
    joint = lax.all_to_all(joint, "seq", 0, 0, tiled=True)
    head_rows = joint[:, :head_width].reshape(nseq, 8, shard_rows, HD)
    head_rows = head_rows.transpose(1, 0, 2, 3).reshape(8, slot_total, HD)
    head_q, head_k, head_v = head_rows[0:2], head_rows[2:5], head_rows[5:8]
    key_ids = jnp.arange(2 * slot_total)
    live_home = key_ids[:slot_total] < own_lengths[0]
    live_shared = key_ids < jnp.where(
        key_ids < slot_total, own_lengths[1], slot_total + pair_lengths[1]
    )
    home_out = head_attend(head_q[0], head_k[0], head_v[0], live_home)
    shared_out = head_attend(
        head_q[1],
        head_k[1:3].reshape(2 * slot_total, HD),
        head_v[1:3].reshape(2 * slot_total, HD),
        live_shared,
    )
    head_attn = jnp.stack([home_out, shared_out]).astype(jnp.bfloat16)

    w_half = joint[:, head_width:].reshape(nseq * block_rows, half_width)
    w_other = from_partner(w_half, "cfg", 0)
    w_quarter = jnp.where(
        branch == 0,
        jnp.concatenate([w_half, w_other], 0),
        jnp.concatenate([w_other, w_half], 0),
    )

    me = lax.axis_index("seq")
    gathered = head_attn[None]
    masks = [0]
    for low_bit in (2, 0):
        parts = [gathered]
        grown = list(masks)
        for digit in (1, 2, 3):
            shift = digit << low_bit
            parts.append(lax.ppermute(gathered, "seq", [(i, i ^ shift) for i in range(nseq)]))
            grown += [m ^ shift for m in masks]
        gathered = jnp.concatenate(parts, 0)
        masks = grown
    plane = len(masks)
    assert masks == [swap_digits(i) for i in range(len(masks))]
    my_z = me % plane
    my_x = me // plane
    by_z = jnp.take(gathered, swap_digits(jnp.bitwise_xor(my_z, jnp.arange(plane))), axis=0)
    my_region = my_x % 2
    parts = [lax.dynamic_index_in_dim(by_z, my_region, 1, keepdims=False)]
    sources = [my_x * plane + jnp.arange(plane)]
    for digit in (1, 2, 3):
        shift = digit * plane
        outgoing = lax.dynamic_index_in_dim(by_z[:used], (my_x ^ digit) % 2, 1, keepdims=False)
        pairs = [(i, i ^ shift) for i in range(nseq)]
        if digit == 1:
            block_size = outgoing.size
            both = lax.ppermute(
                jnp.concatenate([outgoing.reshape(-1), w_quarter.reshape(-1)]), "seq", pairs
            )
            parts.append(both[:block_size].reshape(outgoing.shape))
            w_partner = both[block_size:].reshape(w_quarter.shape)
        else:
            parts.append(lax.ppermute(outgoing, "seq", pairs))
        sources.append(jnp.bitwise_xor(my_x, digit) * plane + jnp.arange(used))
    gathered = jnp.concatenate(parts, 0)
    w_cols = jnp.where(
        my_region == 0,
        jnp.concatenate([w_quarter, w_partner], 1),
        jnp.concatenate([w_partner, w_quarter], 1),
    )
    source_head = head_of(jnp.concatenate(sources))
    w_heads = jnp.pad(w_cols.reshape(HEADS, HD, col_width), ((0, 1), (0, 0), (0, 0)))
    w_ordered = jnp.take(w_heads, source_head, axis=0)
    projected_cols = jnp.einsum(
        "isd,idc->sc", gathered, w_ordered, preferred_element_type=jnp.float32
    )
    projected_parts = projected_cols.reshape(nseq, shard_rows, col_width)
    received = lax.all_to_all(projected_parts, "seq", 0, 0, tiled=True)
    projected = received.reshape(2, 2, 16, shard_rows, col_width).transpose(1, 3, 0, 2, 4)
    projected = projected.reshape(2, shard_rows, D)

    item_count = guide.shape[0]
    indicator_mask = (jnp.arange(item_count)[None, :] == item_ids[:, None]).astype(jnp.float32)
    gate_now = jnp.einsum(
        "ri,id->rd", indicator_mask, attn_gate[0], precision=lax.Precision.HIGHEST
    )
    stream = hidden[0, 0].astype(jnp.float32) + gate_now[:, None, :] * projected
    row_mean = jnp.mean(stream, axis=2, keepdims=True)
    centred = stream - row_mean
    row_var = jnp.mean(centred * centred, axis=2, keepdims=True)
    normed = centred * lax.rsqrt(row_var + NORM_EPS)
    selected_entries = jnp.einsum(
        "ub,bkg->ukg", indicator_mask, modulation[0], precision=lax.Precision.HIGHEST
    )
    shaped = (
        normed * (1.0 + selected_entries[:, 1][:, None, :]) + selected_entries[:, 0][:, None, :]
    ).astype(jnp.bfloat16)
    velocity = jnp.einsum("rsd,dc->rsc", shaped, w_final, preferred_element_type=jnp.float32)
    row_slots = lax.axis_index("seq") * shard_rows + jnp.arange(shard_rows)
    live_rows = jnp.stack([row_slots < own_lengths[0], row_slots < own_lengths[1]])
    velocity = jnp.where(live_rows[:, :, None], velocity, jnp.float32(0.0))
    weight_now = jnp.sum(indicator_mask * guide[None, :], axis=1)[:, None, None]
    step_now = jnp.sum(indicator_mask * step_size[None, :], axis=1)[:, None, None]
    latent_part = latent[0]
    part_width = latent_part.shape[2]
    outgoing_velocity = lax.dynamic_slice_in_dim(velocity, (1 - branch) * part_width, part_width, 2)
    own_velocity = lax.dynamic_slice_in_dim(velocity, branch * part_width, part_width, 2)
    other_velocity = from_partner(outgoing_velocity, "cfg", 0)
    is_conditional = branch == 0
    own_weight = jnp.where(is_conditional, weight_now, 1.0 - weight_now)
    other_weight = jnp.where(is_conditional, 1.0 - weight_now, weight_now)
    partial = latent_part - step_now * (own_weight * own_velocity)
    updated = partial - step_now * (other_weight * other_velocity)
    return updated[None]


def solution(mesh):
    placed = (
        P("cfg", "grp", None, "seq", None),
        P("cfg", "grp", None, "seq", None),
        P("cfg", "grp", None, "seq", None),
        P("cfg", "grp", None, "seq", None),
        P("grp", None, "seq", "cfg"),
        P(),
        P(),
        P(("cfg", "seq"), None),
        P("cfg", None, None),
        P("cfg", None, None, None),
        P(),
        P(),
        P(),
    )
    return jax.shard_map(
        shards, mesh=mesh, in_specs=placed, out_specs=P("grp", None, "seq", "cfg"), check_vma=False
    )
```
